32 devices in a mesh: patch: 2 (over x), row: 16 (over z, y, core).
Axes of the slice: x: 2, y: 2, z: 4, core: 2. Of those that a mesh axis runs over, the one named last changes fastest.
Arguments:
- stokes_q: float32 [256, 8192], P(('patch', 'row')), parts along dimension 0, may hold values from -6 to 6
- stokes_u: float32 [256, 8192], P(('patch', 'row')), parts along dimension 0, may hold values from -6 to 6
- wiener_filter: float32 [256, 8192], P('patch', 'row'), parts along dimension 0, may hold values from 0.2 to 2, as said below
- inverse_filter: float32 [256, 8192], P('patch', 'row'), parts along dimension 0, may hold values from 0.2 to 2, as said below
- lens_norm: float32 [256, 8192], P('patch', 'row'), parts along dimension 0, may hold values from 0.5 to 4, as said below
- conv_first: bfloat16 [3, 3, 32, 3], replicated, may hold values from -1.25 to 1.25
- bias_first: float32 [32], replicated, may hold values from -3 to 3
- conv_second: bfloat16 [3, 3, 32, 32], replicated, may hold values from -0.375 to 0.375
- bias_second: float32 [32], replicated, may hold values from -3 to 3
- head_weight: bfloat16 [2, 32], replicated, may hold values from -1 to 1
- head_bias: float32 [2], replicated, may hold values from -3 to 3
- cotangent: bfloat16 [2, 256, 1024], P(None, ('patch', 'row')), parts along dimension 1, may hold values from -0.016479492 to 0.016479492
Outputs:
- delensed: float32 [2, 256, 1024], P(None, ('patch', 'row')), parts along dimension 1
- grad_conv_first: float32 [6, 3, 32, 3], P('patch'), parts along dimension 0
- grad_bias_first: float32 [64], P('patch'), parts along dimension 0
- grad_conv_second: float32 [6, 3, 32, 32], P('patch'), parts along dimension 0
- grad_bias_second: float32 [64], P('patch'), parts along dimension 0
- grad_head: float32 [4, 32], P('patch'), parts along dimension 0
- grad_head_bias: float32 [4], P('patch'), parts along dimension 0
The draws below stay inside these ranges and needn't reach their ends.
There are 2 independent parts, one for each index of `patch`. The reference program is written for one: setup_inputs(seed, part) draws one part's arguments, and reference() takes and returns one part's arrays. A program takes and returns all parts, laid end to end along the dimension named above; an argument that names none is the same for every part. Nothing has to cross between parts.
Inputs may be any that keep to these rules, and one draw needn't show every extreme that they name: `wiener_filter`: even in the wavenumber: entry (i, j) equals entry ((-i) mod 128, (-j) mod 8192). `inverse_filter`: even in the wavenumber: entry (i, j) equals entry ((-i) mod 128, (-j) mod 8192). `lens_norm`: even in the wavenumber: entry (i, j) equals entry ((-i) mod 128, (-j) mod 8192).
All inputs are finite; a program needn't handle non-finite values.
Results may differ from the reference program's by a relative error of at most 0.0085.
Values may be sent and summed in bfloat16 or wider, within the bound.
No kernel may reach another device: no remote copies, remote signals or barrier semaphores. Data moves between devices by JAX's collectives and lax.ppermute only.
A program may use at most 128 MiB of HBM per device.

```python
import jax
import jax.numpy as jnp
from jax import lax

W = 8192
R_DEV = 8
CW = 1024
CH = 32
H = 128
N_ROW = 16


def mirrored(field):
    return jnp.roll(jnp.flip(field, (0, 1)), 1, (0, 1))


def even_field(key, lower, upper):
    base_field = jnp.exp(jax.random.uniform(key, (H, W), jnp.float32, jnp.log(lower), jnp.log(upper)))
    return 0.5 * (base_field + mirrored(base_field))


def draw_wiener_filter(key, part):
    return even_field(jax.random.fold_in(key, 11), 0.2, 2.0)


def draw_inverse_filter(key, part):
    return even_field(jax.random.fold_in(key, 23), 0.2, 2.0)


def draw_lens_norm(key, part):
    return even_field(jax.random.fold_in(key, 37), 0.5, 4.0)


def levels(key, shape, split, least, top_value):
    level = 1.0
    for dim, blocks in split:
        heights = jax.random.uniform(jax.random.fold_in(jax.random.fold_in(key, 6), dim), (blocks,), jnp.float32, least / len(split), top_value / len(split))
        level = level * jnp.repeat(jnp.exp(heights), shape[dim] // blocks).reshape((-1,) + (1,) * (len(shape) - 1 - dim))
    return level


def noise(stream_key, dims, deviation, most, cuts=(), kind=jnp.bfloat16):
    entries = jax.random.normal(stream_key, dims, jnp.float32) * deviation
    if len(cuts) > 0:
        entries = levels(stream_key, dims, cuts, -0.22, 0.18) * entries
    return jnp.clip(entries, min=-most, max=most).astype(kind)


def setup_inputs(seed: int = 0, part: int = 0) -> dict:
    key_list = jax.random.split(jax.random.key(seed), 13)
    part_splits = jax.random.split(jax.random.fold_in(key_list[12], part), 13)
    stokes_q = noise(part_splits[0], (H, W), 1.0, 6.0, ((0, 16),), jnp.float32)
    stokes_u = noise(part_splits[1], (H, W), 1.0, 6.0, ((0, 16),), jnp.float32)
    wiener_filter = draw_wiener_filter(jax.random.fold_in(jax.random.fold_in(key_list[12], part), 71), part)
    inverse_filter = draw_inverse_filter(jax.random.fold_in(jax.random.fold_in(key_list[12], part), 71), part)
    lens_norm = draw_lens_norm(jax.random.fold_in(jax.random.fold_in(key_list[12], part), 71), part)
    conv_first = noise(key_list[5], (3, 3, CH, 3), 27 ** -0.5, 1.25)
    bias_first = noise(key_list[6], (CH,), 0.5, 3.0, (), jnp.float32)
    conv_second = noise(key_list[7], (3, 3, CH, CH), (9 * CH) ** -0.5, 0.375)
    bias_second = noise(key_list[8], (CH,), 0.5, 3.0, (), jnp.float32)
    head_weight = noise(key_list[9], (2, CH), CH ** -0.5, 1.0)
    head_bias = noise(key_list[10], (2,), 0.5, 3.0, (), jnp.float32)
    cotangent = noise(part_splits[11], (2, H, CW), ((R_DEV * N_ROW * CW) ** -0.5), 0.016479492, ((1, 16),))
    return dict(stokes_q=stokes_q, stokes_u=stokes_u, wiener_filter=wiener_filter, inverse_filter=inverse_filter, lens_norm=lens_norm, conv_first=conv_first, bias_first=bias_first, conv_second=conv_second, bias_second=bias_second, head_weight=head_weight, head_bias=head_bias, cotangent=cotangent)


def wavenumber(length):
    position = jnp.arange(length, dtype=jnp.int32)
    middle = length // 2
    shifted = jnp.where(position < middle, position, jnp.where(position == middle, 0, position - length))
    return shifted.astype(jnp.float32) * (2.0 / length)

def silu_slope(values):
    sigmoid = jax.nn.sigmoid(values)
    return sigmoid * (1.0 + values * (1.0 - sigmoid))

def conv_taps(padded, kernel, row_count, col_count):
    summed = jnp.zeros((kernel.shape[2], row_count, col_count), jnp.float32)
    for row_tap in range(3):
        for col_tap in range(3):
            summed = summed + jnp.einsum('ci,irx->crx', kernel[row_tap, col_tap].astype(jnp.float32), padded[:, row_tap:row_tap + row_count, col_tap:col_tap + col_count].astype(jnp.float32))
    return summed

def conv_back(padded, kernel, row_count, col_count):
    summed = jnp.zeros((kernel.shape[3], row_count, col_count), jnp.float32)
    for row_tap in range(3):
        for col_tap in range(3):
            summed = summed + jnp.einsum('ci,crx->irx', kernel[row_tap, col_tap].astype(jnp.float32), padded[:, 2 - row_tap:2 - row_tap + row_count, 2 - col_tap:2 - col_tap + col_count].astype(jnp.float32))
    return summed

def kernel_grad(upstream, padded, row_count, col_count):
    tap_rows = []
    for row_tap in range(3):
        tap_cols = []
        for col_tap in range(3):
            tap_cols.append(jnp.einsum('crx,irx->ci', upstream.astype(jnp.float32), padded[:, row_tap:row_tap + row_count, col_tap:col_tap + col_count].astype(jnp.float32)))
        tap_rows.append(jnp.stack(tap_cols))
    return jnp.stack(tap_rows)

def pad_both(block):
    return jnp.pad(block, ((0, 0), (1, 1), (1, 1)))

def reference(stokes_q, stokes_u, wiener_filter, inverse_filter, lens_norm, conv_first, bias_first, conv_second, bias_second, head_weight, head_bias, cotangent):
    col_freq = wavenumber(W)[None, :]
    row_freq = wavenumber(H)[:, None]
    radius = col_freq * col_freq + row_freq * row_freq
    safe_radius = jnp.where(radius > 0, radius, 1.0)
    cos_twice = (col_freq * col_freq - row_freq * row_freq) / safe_radius
    sin_twice = 2.0 * col_freq * row_freq / safe_radius
    emode = cos_twice * jnp.fft.fft2(stokes_q) + sin_twice * jnp.fft.fft2(stokes_u)
    filtered = jnp.real(jnp.fft.ifft2(inverse_filter * emode))
    wiener_mode = wiener_filter * emode
    gradient_x = jnp.real(jnp.fft.ifft2(1j * col_freq * wiener_mode))
    gradient_y = jnp.real(jnp.fft.ifft2(1j * row_freq * wiener_mode))
    power_x = jnp.fft.fft2(filtered * gradient_x)
    power_y = jnp.fft.fft2(filtered * gradient_y)
    lens_field = jnp.real(jnp.fft.ifft2(-lens_norm * (1j * col_freq * power_x + 1j * row_freq * power_y)))
    band_start = W // 2 - CW // 2
    band_q = stokes_q[:, band_start:band_start + CW]
    band_u = stokes_u[:, band_start:band_start + CW]
    net_input = jnp.stack([lens_field[:, band_start:band_start + CW], band_q, band_u]).astype(jnp.bfloat16)
    padded_input = pad_both(net_input)
    pre_first = conv_taps(padded_input, conv_first, H, CW) + bias_first[:, None, None]
    hidden_first = jax.nn.silu(pre_first).astype(jnp.bfloat16)
    padded_hidden = pad_both(hidden_first)
    pre_second = conv_taps(padded_hidden, conv_second, H, CW) + bias_second[:, None, None]
    hidden_second = jax.nn.silu(pre_second).astype(jnp.bfloat16)
    head_out = jnp.einsum('oc,crx->orx', head_weight.astype(jnp.float32), hidden_second.astype(jnp.float32))
    delensed = jnp.stack([band_q, band_u]) + head_out + head_bias[:, None, None]
    upstream = cotangent.astype(jnp.float32)
    grad_head = jnp.einsum('orx,crx->oc', upstream, hidden_second.astype(jnp.float32))
    grad_head_bias = lax.optimization_barrier(jnp.sum(upstream, axis=(1, 2)))
    back_second = (jnp.einsum('oc,orx->crx', head_weight.astype(jnp.float32), upstream) * silu_slope(pre_second)).astype(jnp.bfloat16)
    grad_conv_second = kernel_grad(back_second, padded_hidden, H, CW)
    grad_bias_second = lax.optimization_barrier(jnp.sum(back_second.astype(jnp.float32), axis=(1, 2)))
    back_first = (conv_back(pad_both(back_second), conv_second, H, CW) * silu_slope(pre_first)).astype(jnp.bfloat16)
    grad_conv_first = kernel_grad(back_first, padded_input, H, CW)
    grad_bias_first = lax.optimization_barrier(jnp.sum(back_first.astype(jnp.float32), axis=(1, 2)))
    return (delensed, grad_conv_first, grad_bias_first, grad_conv_second, grad_bias_second, grad_head, grad_head_bias)
```

```python
import jax
import jax.numpy as jnp
from jax import lax
from jax.sharding import PartitionSpec as P


def padded_2(block, sides, width):
    for axis, dim in sides:
        count = lax.axis_size(axis)
        forward = [(i, i + 1) for i in range(count - 1)]
        backward = [(target, source) for source, target in forward]
        low = lax.ppermute(
            lax.slice_in_dim(block, block.shape[dim] - width, None, axis=dim), axis, forward
        )
        high = lax.ppermute(lax.slice_in_dim(block, 0, width, axis=dim), axis, backward)
        block = jnp.concatenate([low, block, high], axis=dim)
    return block


def wavenumber(position, length):
    middle = length // 2
    shifted = jnp.where(
        position < middle, position, jnp.where(position == middle, 0, position - length)
    )
    return shifted.astype(jnp.float32) * (2.0 / length)


def to_pencils(spectra):
    count = spectra.shape[0]
    planes = jnp.concatenate([jnp.real(spectra), jnp.imag(spectra)], axis=0)
    arrived = lax.all_to_all(planes, "row", split_axis=2, concat_axis=1, tiled=True)
    return lax.complex(arrived[:count], arrived[count:])


def to_rows(spectra):
    count = spectra.shape[0]
    planes = jnp.concatenate([jnp.real(spectra), jnp.imag(spectra)], axis=0)
    arrived = lax.all_to_all(planes, "row", split_axis=1, concat_axis=2, tiled=True)
    return lax.complex(arrived[:count], arrived[count:])


def forward_grid(fields):
    rows = jnp.fft.fft(fields.astype(jnp.complex64), axis=-1)
    return jnp.fft.fft(to_pencils(rows), axis=-2)


def inverse_grid(spectra):
    cols = jnp.fft.ifft(spectra, axis=-2)
    return jnp.fft.ifft(to_rows(cols), axis=-1)


def row_rim(block, depth):
    return padded_2(block, (("row", 1),), depth)


def pad_columns(block):
    return jnp.pad(block, ((0, 0), (0, 0), (1, 1)))


def conv_taps(rows_wide, kernel):
    out_rows = rows_wide.shape[1] - 2
    out_cols = rows_wide.shape[2]
    padded = pad_columns(rows_wide)
    summed = None
    for row_tap in range(3):
        for col_tap in range(3):
            partial_value = jnp.einsum(
                "ci,irx->crx",
                kernel[row_tap, col_tap],
                padded[:, row_tap : row_tap + out_rows, col_tap : col_tap + out_cols],
                preferred_element_type=jnp.float32,
            )
            summed = partial_value if summed is None else summed + partial_value
    return summed


def conv_back(rows_wide, kernel):
    out_rows = rows_wide.shape[1] - 2
    out_cols = rows_wide.shape[2]
    padded = pad_columns(rows_wide)
    summed = None
    for row_tap in range(3):
        for col_tap in range(3):
            partial_value = jnp.einsum(
                "ci,crx->irx",
                kernel[row_tap, col_tap],
                padded[
                    :, 2 - row_tap : 2 - row_tap + out_rows, 2 - col_tap : 2 - col_tap + out_cols
                ],
                preferred_element_type=jnp.float32,
            )
            summed = partial_value if summed is None else summed + partial_value
    return summed


def kernel_grad(upstream, rows_wide):
    out_rows = upstream.shape[1]
    out_cols = upstream.shape[2]
    padded = pad_columns(rows_wide)
    tap_rows = []
    for row_tap in range(3):
        tap_cols = []
        for col_tap in range(3):
            tap_cols.append(
                jnp.einsum(
                    "crx,irx->ci",
                    upstream,
                    padded[:, row_tap : row_tap + out_rows, col_tap : col_tap + out_cols],
                    preferred_element_type=jnp.float32,
                )
            )
        tap_rows.append(jnp.stack(tap_cols))
    return jnp.stack(tap_rows)


def silu_slope(values):
    sigmoid = jax.nn.sigmoid(values)
    return sigmoid * (1.0 + values * (1.0 - sigmoid))


def per_device(
    stokes_q,
    stokes_u,
    wiener_filter,
    inverse_filter,
    lens_norm,
    conv_first,
    bias_first,
    conv_second,
    bias_second,
    head_weight,
    head_bias,
    cotangent,
):
    row_count, col_count = stokes_q.shape
    devices = lax.axis_size("row")
    height = row_count * devices
    pencil = col_count // devices
    band_cols = cotangent.shape[2]
    column_ids = lax.axis_index("row") * pencil + jnp.arange(pencil, dtype=jnp.int32)
    col_freq = wavenumber(column_ids, col_count)[None, :]
    row_freq = wavenumber(jnp.arange(height, dtype=jnp.int32), height)[:, None]
    radius = col_freq * col_freq + row_freq * row_freq
    safe_radius = jnp.where(radius > 0, radius, 1.0)
    cos_twice = (col_freq * col_freq - row_freq * row_freq) / safe_radius
    sin_twice = 2.0 * col_freq * row_freq / safe_radius
    stokes_spec = forward_grid(jnp.stack([stokes_q, stokes_u]))
    emode = cos_twice * stokes_spec[0] + sin_twice * stokes_spec[1]
    wiener_mode = wiener_filter * emode
    packed = inverse_filter * emode - col_freq * wiener_mode
    slope_y = lax.complex(-row_freq * jnp.imag(wiener_mode), row_freq * jnp.real(wiener_mode))
    fields = inverse_grid(jnp.stack([packed, slope_y]))
    filtered = jnp.real(fields[0])
    gradient_x = jnp.imag(fields[0])
    gradient_y = jnp.real(fields[1])
    power = forward_grid(jnp.stack([filtered * gradient_x, filtered * gradient_y]))
    mixed = col_freq * power[0] + row_freq * power[1]
    lens_spec = lax.complex(lens_norm * jnp.imag(mixed), -lens_norm * jnp.real(mixed))
    lens_real = jnp.real(inverse_grid(lens_spec[None])[0])
    band_start = col_count // 2 - band_cols // 2
    band_q = stokes_q[:, band_start : band_start + band_cols]
    band_u = stokes_u[:, band_start : band_start + band_cols]
    net_input = jnp.stack(
        [lens_real[:, band_start : band_start + band_cols], band_q, band_u]
    ).astype(jnp.bfloat16)
    input_edge = row_rim(net_input, 1)
    pre_first = conv_taps(input_edge, conv_first) + bias_first[:, None, None]
    hidden_wide = row_rim(jax.nn.silu(pre_first).astype(jnp.bfloat16), 1)
    pre_second = conv_taps(hidden_wide, conv_second) + bias_second[:, None, None]
    hidden_second = jax.nn.silu(pre_second).astype(jnp.bfloat16)
    head_out = jnp.einsum(
        "oc,crx->orx", head_weight, hidden_second, preferred_element_type=jnp.float32
    )
    delensed = jnp.stack([band_q, band_u]) + head_out + head_bias[:, None, None]
    grad_head = jnp.einsum(
        "orx,crx->oc", cotangent, hidden_second, preferred_element_type=jnp.float32
    )
    grad_head_bias = jnp.sum(cotangent.astype(jnp.float32), axis=(1, 2))
    through_head = jnp.einsum(
        "oc,orx->crx", head_weight, cotangent, preferred_element_type=jnp.float32
    )
    back_second = (through_head * silu_slope(pre_second)).astype(jnp.bfloat16)
    grad_conv_second = kernel_grad(back_second, hidden_wide)
    grad_bias_second = jnp.sum(back_second.astype(jnp.float32), axis=(1, 2))
    back_wide = row_rim(back_second, 1)
    back_first = (conv_back(back_wide, conv_second) * silu_slope(pre_first)).astype(jnp.bfloat16)
    grad_conv_first = kernel_grad(back_first, input_edge)
    grad_bias_first = jnp.sum(back_first.astype(jnp.float32), axis=(1, 2))
    grads = (
        grad_conv_first,
        grad_bias_first,
        grad_conv_second,
        grad_bias_second,
        grad_head,
        grad_head_bias,
    )
    flat = lax.psum(jnp.concatenate([g.reshape(-1) for g in grads]), "row")
    summed_grads = []
    offset = 0
    for g in grads:
        summed_grads.append(flat[offset : offset + g.size].reshape(g.shape))
        offset += g.size
    return (delensed, *summed_grads)


def solution(mesh):
    return jax.shard_map(
        per_device,
        mesh=mesh,
        in_specs=(
            P(("patch", "row"), None),
            P(("patch", "row"), None),
            P("patch", "row"),
            P("patch", "row"),
            P("patch", "row"),
            P(),
            P(),
            P(),
            P(),
            P(),
            P(),
            P(None, ("patch", "row"), None),
        ),
        out_specs=(
            P(None, ("patch", "row"), None),
            P("patch", None, None, None),
            P("patch"),
            P("patch", None, None, None),
            P("patch"),
            P("patch", None),
            P("patch"),
        ),
        check_vma=False,
    )
```

```python
import jax
import jax.numpy as jnp
from jax import lax
from jax.sharding import PartitionSpec as P


def padded_2(block, sides, width):
    for axis, dim in sides:
        count = lax.axis_size(axis)
        forward = [(i, i + 1) for i in range(count - 1)]
        backward = [(target, source) for source, target in forward]
        low = lax.ppermute(
            lax.slice_in_dim(block, block.shape[dim] - width, None, axis=dim), axis, forward
        )
        high = lax.ppermute(lax.slice_in_dim(block, 0, width, axis=dim), axis, backward)
        block = jnp.concatenate([low, block, high], axis=dim)
    return block


def wavenumber(position, length):
    middle = length // 2
    shifted = jnp.where(
        position < middle, position, jnp.where(position == middle, 0, position - length)
    )
    return shifted.astype(jnp.float32) * (2.0 / length)


def to_pencils(spectra):
    count, rows, cols = spectra.shape
    devices = lax.axis_size("row")
    planes = jnp.concatenate([jnp.real(spectra), jnp.imag(spectra)], axis=0)
    blocks = planes.reshape(2 * count, rows, devices, cols // devices).transpose(2, 0, 1, 3)
    arrived = lax.all_to_all(blocks, "row", split_axis=0, concat_axis=0, tiled=True)
    arrived = arrived.transpose(1, 0, 2, 3).reshape(2 * count, devices * rows, cols // devices)
    return lax.complex(arrived[:count], arrived[count:])


def to_rows(spectra):
    count = spectra.shape[0]
    planes = jnp.concatenate([jnp.real(spectra), jnp.imag(spectra)], axis=0)
    arrived = lax.all_to_all(planes, "row", split_axis=1, concat_axis=2, tiled=True)
    return lax.complex(arrived[:count], arrived[count:])


def butterfly_sum(values, axis):
    count = lax.axis_size(axis)
    if count & (count - 1):
        return lax.psum(values, axis)
    stride = 1
    while stride < count:
        pairs = [(i, i ^ stride) for i in range(count)]
        values = values + lax.ppermute(values, axis, pairs)
        stride *= 2
    return values


def forward_grid(fields):
    rows = jnp.fft.fft(fields.astype(jnp.complex64), axis=-1)
    return jnp.fft.fft(to_pencils(rows), axis=-2)


def inverse_grid(spectra):
    cols = jnp.fft.ifft(spectra, axis=-2)
    return jnp.fft.ifft(to_rows(cols), axis=-1)


def row_rim(block, depth):
    return padded_2(block, (("row", 1),), depth)


def pad_columns(block):
    return jnp.pad(block, ((0, 0), (0, 0), (1, 1)))


def conv_taps(rows_wide, kernel):
    out_rows = rows_wide.shape[1] - 2
    out_cols = rows_wide.shape[2]
    padded = pad_columns(rows_wide)
    summed = None
    for row_tap in range(3):
        for col_tap in range(3):
            partial_value = jnp.einsum(
                "ci,irx->crx",
                kernel[row_tap, col_tap],
                padded[:, row_tap : row_tap + out_rows, col_tap : col_tap + out_cols],
                preferred_element_type=jnp.float32,
            )
            summed = partial_value if summed is None else summed + partial_value
    return summed


def conv_back(rows_wide, kernel):
    out_rows = rows_wide.shape[1] - 2
    out_cols = rows_wide.shape[2]
    padded = pad_columns(rows_wide)
    summed = None
    for row_tap in range(3):
        for col_tap in range(3):
            partial_value = jnp.einsum(
                "ci,crx->irx",
                kernel[row_tap, col_tap],
                padded[
                    :, 2 - row_tap : 2 - row_tap + out_rows, 2 - col_tap : 2 - col_tap + out_cols
                ],
                preferred_element_type=jnp.float32,
            )
            summed = partial_value if summed is None else summed + partial_value
    return summed


def kernel_grad(upstream, rows_wide):
    out_rows = upstream.shape[1]
    out_cols = upstream.shape[2]
    padded = pad_columns(rows_wide)
    tap_rows = []
    for row_tap in range(3):
        tap_cols = []
        for col_tap in range(3):
            tap_cols.append(
                jnp.einsum(
                    "crx,irx->ci",
                    upstream,
                    padded[:, row_tap : row_tap + out_rows, col_tap : col_tap + out_cols],
                    preferred_element_type=jnp.float32,
                )
            )
        tap_rows.append(jnp.stack(tap_cols))
    return jnp.stack(tap_rows)


def silu_slope(values):
    sigmoid = jax.nn.sigmoid(values)
    return sigmoid * (1.0 + values * (1.0 - sigmoid))


def per_device(
    stokes_q,
    stokes_u,
    wiener_filter,
    inverse_filter,
    lens_norm,
    conv_first,
    bias_first,
    conv_second,
    bias_second,
    head_weight,
    head_bias,
    cotangent,
):
    row_count, col_count = stokes_q.shape
    devices = lax.axis_size("row")
    height = row_count * devices
    pencil = col_count // devices
    band_cols = cotangent.shape[2]
    column_ids = lax.axis_index("row") * pencil + jnp.arange(pencil, dtype=jnp.int32)
    col_freq = wavenumber(column_ids, col_count)[None, :]
    row_freq = wavenumber(jnp.arange(height, dtype=jnp.int32), height)[:, None]
    radius = col_freq * col_freq + row_freq * row_freq
    safe_radius = jnp.where(radius > 0, radius, 1.0)
    cos_twice = (col_freq * col_freq - row_freq * row_freq) / safe_radius
    sin_twice = 2.0 * col_freq * row_freq / safe_radius
    stokes_spec = forward_grid(jnp.stack([stokes_q, stokes_u]))
    emode = cos_twice * stokes_spec[0] + sin_twice * stokes_spec[1]
    wiener_mode = wiener_filter * emode
    packed = inverse_filter * emode - col_freq * wiener_mode
    slope_y = lax.complex(-row_freq * jnp.imag(wiener_mode), row_freq * jnp.real(wiener_mode))
    fields = inverse_grid(jnp.stack([packed, slope_y]))
    filtered = jnp.real(fields[0])
    gradient_x = jnp.imag(fields[0])
    gradient_y = jnp.real(fields[1])
    power = forward_grid(jnp.stack([filtered * gradient_x, filtered * gradient_y]))
    mixed = col_freq * power[0] + row_freq * power[1]
    lens_spec = lax.complex(lens_norm * jnp.imag(mixed), -lens_norm * jnp.real(mixed))
    lens_real = jnp.real(inverse_grid(lens_spec[None])[0])
    band_start = col_count // 2 - band_cols // 2
    band_q = stokes_q[:, band_start : band_start + band_cols]
    band_u = stokes_u[:, band_start : band_start + band_cols]
    net_input = jnp.stack(
        [lens_real[:, band_start : band_start + band_cols], band_q, band_u]
    ).astype(jnp.bfloat16)
    input_edge = row_rim(net_input, 1)
    pre_first = conv_taps(input_edge, conv_first) + bias_first[:, None, None]
    hidden_wide = row_rim(jax.nn.silu(pre_first).astype(jnp.bfloat16), 1)
    pre_second = conv_taps(hidden_wide, conv_second) + bias_second[:, None, None]
    hidden_second = jax.nn.silu(pre_second).astype(jnp.bfloat16)
    head_out = jnp.einsum(
        "oc,crx->orx", head_weight, hidden_second, preferred_element_type=jnp.float32
    )
    delensed = jnp.stack([band_q, band_u]) + head_out + head_bias[:, None, None]
    grad_head = jnp.einsum(
        "orx,crx->oc", cotangent, hidden_second, preferred_element_type=jnp.float32
    )
    grad_head_bias = jnp.sum(cotangent.astype(jnp.float32), axis=(1, 2))
    through_head = jnp.einsum(
        "oc,orx->crx", head_weight, cotangent, preferred_element_type=jnp.float32
    )
    back_second = (through_head * silu_slope(pre_second)).astype(jnp.bfloat16)
    grad_conv_second = kernel_grad(back_second, hidden_wide)
    grad_bias_second = jnp.sum(back_second.astype(jnp.float32), axis=(1, 2))
    back_wide = row_rim(back_second, 1)
    back_first = (conv_back(back_wide, conv_second) * silu_slope(pre_first)).astype(jnp.bfloat16)
    grad_conv_first = kernel_grad(back_first, input_edge)
    grad_bias_first = jnp.sum(back_first.astype(jnp.float32), axis=(1, 2))
    grads = (
        grad_conv_first,
        grad_bias_first,
        grad_conv_second,
        grad_bias_second,
        grad_head,
        grad_head_bias,
    )
    flat = butterfly_sum(jnp.concatenate([g.reshape(-1) for g in grads]), "row")
    summed_grads = []
    offset = 0
    for g in grads:
        summed_grads.append(flat[offset : offset + g.size].reshape(g.shape))
        offset += g.size
    return (delensed, *summed_grads)


def solution(mesh):
    return jax.shard_map(
        per_device,
        mesh=mesh,
        in_specs=(
            P(("patch", "row"), None),
            P(("patch", "row"), None),
            P("patch", "row"),
            P("patch", "row"),
            P("patch", "row"),
            P(),
            P(),
            P(),
            P(),
            P(),
            P(),
            P(None, ("patch", "row"), None),
        ),
        out_specs=(
            P(None, ("patch", "row"), None),
            P("patch", None, None, None),
            P("patch"),
            P("patch", None, None, None),
            P("patch"),
            P("patch", None),
            P("patch"),
        ),
        check_vma=False,
    )
```

```python
import jax
import jax.numpy as jnp
from jax import lax
from jax.sharding import PartitionSpec as P

LINK = jnp.bfloat16


def padded_2(block, sides, width):
    for axis, dim in sides:
        count = lax.axis_size(axis)
        forward = [(i, i + 1) for i in range(count - 1)]
        backward = [(target, source) for source, target in forward]
        low = lax.ppermute(
            lax.slice_in_dim(block, block.shape[dim] - width, None, axis=dim), axis, forward
        )
        high = lax.ppermute(lax.slice_in_dim(block, 0, width, axis=dim), axis, backward)
        block = jnp.concatenate([low, block, high], axis=dim)
    return block


def wavenumber(position, length):
    middle = length // 2
    shifted = jnp.where(
        position < middle, position, jnp.where(position == middle, 0, position - length)
    )
    return shifted.astype(jnp.float32) * (2.0 / length)


def to_pencils(spectra):
    count, rows, cols = spectra.shape
    devices = lax.axis_size("row")
    planes = jnp.concatenate([jnp.real(spectra), jnp.imag(spectra)], axis=0).astype(LINK)
    blocks = planes.reshape(2 * count, rows, devices, cols // devices).transpose(2, 0, 1, 3)
    arrived = lax.all_to_all(blocks, "row", split_axis=0, concat_axis=0, tiled=True)
    arrived = arrived.transpose(1, 0, 2, 3).reshape(2 * count, devices * rows, cols // devices)
    arrived = arrived.astype(jnp.float32)
    return lax.complex(arrived[:count], arrived[count:])


def to_rows(spectra):
    count = spectra.shape[0]
    planes = jnp.concatenate([jnp.real(spectra), jnp.imag(spectra)], axis=0).astype(LINK)
    arrived = lax.all_to_all(planes, "row", split_axis=1, concat_axis=2, tiled=True)
    arrived = arrived.astype(jnp.float32)
    return lax.complex(arrived[:count], arrived[count:])


def butterfly_sum(values, axis):
    count = lax.axis_size(axis)
    if count & (count - 1):
        return lax.psum(values, axis)
    stride = 1
    while stride < count:
        pairs = [(i, i ^ stride) for i in range(count)]
        values = values + lax.ppermute(values, axis, pairs)
        stride *= 2
    return values


def forward_grid(fields):
    rows = jnp.fft.fft(fields.astype(jnp.complex64), axis=-1)
    return jnp.fft.fft(to_pencils(rows), axis=-2)


def inverse_grid(spectra):
    cols = jnp.fft.ifft(spectra, axis=-2)
    return jnp.fft.ifft(to_rows(cols), axis=-1)


def row_rim(block, depth):
    return padded_2(block, (("row", 1),), depth)


def pad_columns(block):
    return jnp.pad(block, ((0, 0), (0, 0), (1, 1)))


def conv_taps(rows_wide, kernel):
    out_rows = rows_wide.shape[1] - 2
    out_cols = rows_wide.shape[2]
    padded = pad_columns(rows_wide)
    summed = None
    for row_tap in range(3):
        for col_tap in range(3):
            partial_value = jnp.einsum(
                "ci,irx->crx",
                kernel[row_tap, col_tap],
                padded[:, row_tap : row_tap + out_rows, col_tap : col_tap + out_cols],
                preferred_element_type=jnp.float32,
            )
            summed = partial_value if summed is None else summed + partial_value
    return summed


def conv_back(rows_wide, kernel):
    out_rows = rows_wide.shape[1] - 2
    out_cols = rows_wide.shape[2]
    padded = pad_columns(rows_wide)
    summed = None
    for row_tap in range(3):
        for col_tap in range(3):
            partial_value = jnp.einsum(
                "ci,crx->irx",
                kernel[row_tap, col_tap],
                padded[
                    :, 2 - row_tap : 2 - row_tap + out_rows, 2 - col_tap : 2 - col_tap + out_cols
                ],
                preferred_element_type=jnp.float32,
            )
            summed = partial_value if summed is None else summed + partial_value
    return summed


def kernel_grad(upstream, rows_wide):
    out_rows = upstream.shape[1]
    out_cols = upstream.shape[2]
    padded = pad_columns(rows_wide)
    tap_rows = []
    for row_tap in range(3):
        tap_cols = []
        for col_tap in range(3):
            tap_cols.append(
                jnp.einsum(
                    "crx,irx->ci",
                    upstream,
                    padded[:, row_tap : row_tap + out_rows, col_tap : col_tap + out_cols],
                    preferred_element_type=jnp.float32,
                )
            )
        tap_rows.append(jnp.stack(tap_cols))
    return jnp.stack(tap_rows)


def silu_slope(values):
    sigmoid = jax.nn.sigmoid(values)
    return sigmoid * (1.0 + values * (1.0 - sigmoid))


def per_device(
    stokes_q,
    stokes_u,
    wiener_filter,
    inverse_filter,
    lens_norm,
    conv_first,
    bias_first,
    conv_second,
    bias_second,
    head_weight,
    head_bias,
    cotangent,
):
    row_count, col_count = stokes_q.shape
    devices = lax.axis_size("row")
    height = row_count * devices
    pencil = col_count // devices
    band_cols = cotangent.shape[2]
    column_ids = lax.axis_index("row") * pencil + jnp.arange(pencil, dtype=jnp.int32)
    col_freq = wavenumber(column_ids, col_count)[None, :]
    row_freq = wavenumber(jnp.arange(height, dtype=jnp.int32), height)[:, None]
    radius = col_freq * col_freq + row_freq * row_freq
    safe_radius = jnp.where(radius > 0, radius, 1.0)
    cos_twice = (col_freq * col_freq - row_freq * row_freq) / safe_radius
    sin_twice = 2.0 * col_freq * row_freq / safe_radius
    stokes_spec = forward_grid(jnp.stack([stokes_q, stokes_u]))
    emode = cos_twice * stokes_spec[0] + sin_twice * stokes_spec[1]
    wiener_mode = wiener_filter * emode
    packed = inverse_filter * emode - col_freq * wiener_mode
    slope_y = lax.complex(-row_freq * jnp.imag(wiener_mode), row_freq * jnp.real(wiener_mode))
    fields = inverse_grid(jnp.stack([packed, slope_y]))
    filtered = jnp.real(fields[0])
    gradient_x = jnp.imag(fields[0])
    gradient_y = jnp.real(fields[1])
    power = forward_grid(jnp.stack([filtered * gradient_x, filtered * gradient_y]))
    mixed = col_freq * power[0] + row_freq * power[1]
    lens_spec = lax.complex(lens_norm * jnp.imag(mixed), -lens_norm * jnp.real(mixed))
    lens_real = jnp.real(inverse_grid(lens_spec[None])[0])
    band_start = col_count // 2 - band_cols // 2
    band_q = stokes_q[:, band_start : band_start + band_cols]
    band_u = stokes_u[:, band_start : band_start + band_cols]
    net_input = jnp.stack(
        [lens_real[:, band_start : band_start + band_cols], band_q, band_u]
    ).astype(jnp.bfloat16)
    input_edge = row_rim(net_input, 1)
    pre_first = conv_taps(input_edge, conv_first) + bias_first[:, None, None]
    hidden_wide = row_rim(jax.nn.silu(pre_first).astype(jnp.bfloat16), 1)
    pre_second = conv_taps(hidden_wide, conv_second) + bias_second[:, None, None]
    hidden_second = jax.nn.silu(pre_second).astype(jnp.bfloat16)
    head_out = jnp.einsum(
        "oc,crx->orx", head_weight, hidden_second, preferred_element_type=jnp.float32
    )
    delensed = jnp.stack([band_q, band_u]) + head_out + head_bias[:, None, None]
    grad_head = jnp.einsum(
        "orx,crx->oc", cotangent, hidden_second, preferred_element_type=jnp.float32
    )
    grad_head_bias = jnp.sum(cotangent.astype(jnp.float32), axis=(1, 2))
    through_head = jnp.einsum(
        "oc,orx->crx", head_weight, cotangent, preferred_element_type=jnp.float32
    )
    back_second = (through_head * silu_slope(pre_second)).astype(jnp.bfloat16)
    grad_conv_second = kernel_grad(back_second, hidden_wide)
    grad_bias_second = jnp.sum(back_second.astype(jnp.float32), axis=(1, 2))
    back_wide = row_rim(back_second, 1)
    back_first = (conv_back(back_wide, conv_second) * silu_slope(pre_first)).astype(jnp.bfloat16)
    grad_conv_first = kernel_grad(back_first, input_edge)
    grad_bias_first = jnp.sum(back_first.astype(jnp.float32), axis=(1, 2))
    grads = (
        grad_conv_first,
        grad_bias_first,
        grad_conv_second,
        grad_bias_second,
        grad_head,
        grad_head_bias,
    )
    flat = butterfly_sum(jnp.concatenate([g.reshape(-1) for g in grads]), "row")
    summed_grads = []
    offset = 0
    for g in grads:
        summed_grads.append(flat[offset : offset + g.size].reshape(g.shape))
        offset += g.size
    return (delensed, *summed_grads)


def solution(mesh):
    return jax.shard_map(
        per_device,
        mesh=mesh,
        in_specs=(
            P(("patch", "row"), None),
            P(("patch", "row"), None),
            P("patch", "row"),
            P("patch", "row"),
            P("patch", "row"),
            P(),
            P(),
            P(),
            P(),
            P(),
            P(),
            P(None, ("patch", "row"), None),
        ),
        out_specs=(
            P(None, ("patch", "row"), None),
            P("patch", None, None, None),
            P("patch"),
            P("patch", None, None, None),
            P("patch"),
            P("patch", None),
            P("patch"),
        ),
        check_vma=False,
    )
```

```python
import jax
import jax.numpy as jnp
from jax import lax
from jax.sharding import PartitionSpec as P

LINK = jnp.bfloat16


def padded_2(block, sides, width):
    for axis, dim in sides:
        count = lax.axis_size(axis)
        forward = [(i, i + 1) for i in range(count - 1)]
        backward = [(target, source) for source, target in forward]
        low = lax.ppermute(
            lax.slice_in_dim(block, block.shape[dim] - width, None, axis=dim), axis, forward
        )
        high = lax.ppermute(lax.slice_in_dim(block, 0, width, axis=dim), axis, backward)
        block = jnp.concatenate([low, block, high], axis=dim)
    return block


def wavenumber(position, length):
    middle = length // 2
    shifted = jnp.where(
        position < middle, position, jnp.where(position == middle, 0, position - length)
    )
    return shifted.astype(jnp.float32) * (2.0 / length)


def to_pencils(spectra):
    count, rows, cols = spectra.shape
    devices = lax.axis_size("row")
    planes = jnp.concatenate([jnp.real(spectra), jnp.imag(spectra)], axis=0).astype(LINK)
    blocks = planes.reshape(2 * count, rows, devices, cols // devices).transpose(2, 0, 1, 3)
    arrived = lax.all_to_all(blocks, "row", split_axis=0, concat_axis=0, tiled=True)
    arrived = arrived.transpose(1, 0, 2, 3).reshape(2 * count, devices * rows, cols // devices)
    arrived = arrived.astype(jnp.float32)
    return lax.complex(arrived[:count], arrived[count:])


def to_rows(spectra):
    count = spectra.shape[0]
    planes = jnp.concatenate([jnp.real(spectra), jnp.imag(spectra)], axis=0).astype(LINK)
    arrived = lax.all_to_all(planes, "row", split_axis=1, concat_axis=2, tiled=True)
    arrived = arrived.astype(jnp.float32)
    return lax.complex(arrived[:count], arrived[count:])


def butterfly_sum(values, axis):
    count = lax.axis_size(axis)
    if count & (count - 1):
        return lax.psum(values, axis)
    stride = 1
    while stride < count:
        pairs = [(i, i ^ stride) for i in range(count)]
        values = values + lax.ppermute(values, axis, pairs)
        stride *= 2
    return values


def flat_sum(tensors):
    flat = butterfly_sum(jnp.concatenate([t.reshape(-1) for t in tensors]), "row")
    summed = []
    offset = 0
    for t in tensors:
        summed.append(flat[offset : offset + t.size].reshape(t.shape))
        offset += t.size
    return summed


def forward_grid(fields):
    rows = jnp.fft.fft(fields.astype(jnp.complex64), axis=-1)
    return jnp.fft.fft(to_pencils(rows), axis=-2)


def inverse_grid(spectra):
    cols = jnp.fft.ifft(spectra, axis=-2)
    return jnp.fft.ifft(to_rows(cols), axis=-1)


def row_rim(block, depth):
    return padded_2(block, (("row", 1),), depth)


def pad_columns(block):
    return jnp.pad(block, ((0, 0), (0, 0), (1, 1)))


def conv_taps(rows_wide, kernel):
    out_rows = rows_wide.shape[1] - 2
    out_cols = rows_wide.shape[2]
    padded = pad_columns(rows_wide)
    summed = None
    for row_tap in range(3):
        for col_tap in range(3):
            partial_value = jnp.einsum(
                "ci,irx->crx",
                kernel[row_tap, col_tap],
                padded[:, row_tap : row_tap + out_rows, col_tap : col_tap + out_cols],
                preferred_element_type=jnp.float32,
            )
            summed = partial_value if summed is None else summed + partial_value
    return summed


def conv_back(rows_wide, kernel):
    out_rows = rows_wide.shape[1] - 2
    out_cols = rows_wide.shape[2]
    padded = pad_columns(rows_wide)
    summed = None
    for row_tap in range(3):
        for col_tap in range(3):
            partial_value = jnp.einsum(
                "ci,crx->irx",
                kernel[row_tap, col_tap],
                padded[
                    :, 2 - row_tap : 2 - row_tap + out_rows, 2 - col_tap : 2 - col_tap + out_cols
                ],
                preferred_element_type=jnp.float32,
            )
            summed = partial_value if summed is None else summed + partial_value
    return summed


def kernel_grad(upstream, rows_wide):
    out_rows = upstream.shape[1]
    out_cols = upstream.shape[2]
    padded = pad_columns(rows_wide)
    tap_rows = []
    for row_tap in range(3):
        tap_cols = []
        for col_tap in range(3):
            tap_cols.append(
                jnp.einsum(
                    "crx,irx->ci",
                    upstream,
                    padded[:, row_tap : row_tap + out_rows, col_tap : col_tap + out_cols],
                    preferred_element_type=jnp.float32,
                )
            )
        tap_rows.append(jnp.stack(tap_cols))
    return jnp.stack(tap_rows)


def silu_slope(values):
    sigmoid = jax.nn.sigmoid(values)
    return sigmoid * (1.0 + values * (1.0 - sigmoid))


def per_device(
    stokes_q,
    stokes_u,
    wiener_filter,
    inverse_filter,
    lens_norm,
    conv_first,
    bias_first,
    conv_second,
    bias_second,
    head_weight,
    head_bias,
    cotangent,
):
    row_count, col_count = stokes_q.shape
    devices = lax.axis_size("row")
    height = row_count * devices
    pencil = col_count // devices
    band_cols = cotangent.shape[2]
    column_ids = lax.axis_index("row") * pencil + jnp.arange(pencil, dtype=jnp.int32)
    col_freq = wavenumber(column_ids, col_count)[None, :]
    row_freq = wavenumber(jnp.arange(height, dtype=jnp.int32), height)[:, None]
    radius = col_freq * col_freq + row_freq * row_freq
    safe_radius = jnp.where(radius > 0, radius, 1.0)
    cos_twice = (col_freq * col_freq - row_freq * row_freq) / safe_radius
    sin_twice = 2.0 * col_freq * row_freq / safe_radius
    stokes_spec = forward_grid(jnp.stack([stokes_q, stokes_u]))
    emode = cos_twice * stokes_spec[0] + sin_twice * stokes_spec[1]
    wiener_mode = wiener_filter * emode
    packed = inverse_filter * emode - col_freq * wiener_mode
    slope_y = lax.complex(-row_freq * jnp.imag(wiener_mode), row_freq * jnp.real(wiener_mode))
    fields = inverse_grid(jnp.stack([packed, slope_y]))
    filtered = jnp.real(fields[0])
    gradient_x = jnp.imag(fields[0])
    gradient_y = jnp.real(fields[1])
    power = forward_grid(jnp.stack([filtered * gradient_x, filtered * gradient_y]))
    mixed = col_freq * power[0] + row_freq * power[1]
    lens_spec = lax.complex(lens_norm * jnp.imag(mixed), -lens_norm * jnp.real(mixed))
    lens_real = jnp.real(inverse_grid(lens_spec[None])[0])
    band_start = col_count // 2 - band_cols // 2
    band_q = stokes_q[:, band_start : band_start + band_cols]
    band_u = stokes_u[:, band_start : band_start + band_cols]
    stokes_wide = row_rim(jnp.stack([band_q, band_u]).astype(jnp.bfloat16), 3)
    cotangent_wide = row_rim(cotangent, 1)
    lens_band = lens_real[:, band_start : band_start + band_cols]
    lens_wide = row_rim(lens_band.astype(jnp.bfloat16)[None], 3)
    input_wide = jnp.concatenate([lens_wide, stokes_wide], axis=0)
    pre_first = conv_taps(input_wide, conv_first) + bias_first[:, None, None]
    global_rows = lax.axis_index("row") * row_count + jnp.arange(-2, row_count + 2)
    inside = (global_rows >= 0) & (global_rows < height)
    hidden_wide = jnp.where(inside[None, :, None], jax.nn.silu(pre_first), 0.0).astype(
        jnp.bfloat16
    )
    pre_second = conv_taps(hidden_wide, conv_second) + bias_second[:, None, None]
    hidden_second = jax.nn.silu(pre_second[:, 1:-1]).astype(jnp.bfloat16)
    head_out = jnp.einsum(
        "oc,crx->orx", head_weight, hidden_second, preferred_element_type=jnp.float32
    )
    delensed = jnp.stack([band_q, band_u]) + head_out + head_bias[:, None, None]
    grad_head = jnp.einsum(
        "orx,crx->oc", cotangent, hidden_second, preferred_element_type=jnp.float32
    )
    grad_head_bias = jnp.sum(cotangent.astype(jnp.float32), axis=(1, 2))
    through_head = jnp.einsum(
        "oc,orx->crx", head_weight, cotangent_wide, preferred_element_type=jnp.float32
    )
    back_wide = (through_head * silu_slope(pre_second)).astype(jnp.bfloat16)
    back_second = back_wide[:, 1:-1]
    grad_conv_second = kernel_grad(back_second, hidden_wide[:, 1:-1])
    grad_bias_second = jnp.sum(back_second.astype(jnp.float32), axis=(1, 2))
    early = flat_sum((grad_conv_second, grad_bias_second, grad_head, grad_head_bias))
    back_first = (
        conv_back(back_wide, conv_second) * silu_slope(pre_first[:, 2:-2])
    ).astype(jnp.bfloat16)
    grad_conv_first = kernel_grad(back_first, input_wide[:, 2:-2])
    grad_bias_first = jnp.sum(back_first.astype(jnp.float32), axis=(1, 2))
    late = flat_sum((grad_conv_first, grad_bias_first))
    return (delensed, *late, *early)


def solution(mesh):
    return jax.shard_map(
        per_device,
        mesh=mesh,
        in_specs=(
            P(("patch", "row"), None),
            P(("patch", "row"), None),
            P("patch", "row"),
            P("patch", "row"),
            P("patch", "row"),
            P(),
            P(),
            P(),
            P(),
            P(),
            P(),
            P(None, ("patch", "row"), None),
        ),
        out_specs=(
            P(None, ("patch", "row"), None),
            P("patch", None, None, None),
            P("patch"),
            P("patch", None, None, None),
            P("patch"),
            P("patch", None),
            P("patch"),
        ),
        check_vma=False,
    )
```

```python
import jax
import jax.numpy as jnp
from jax import lax
from jax.sharding import PartitionSpec as P

LINK = jnp.bfloat16


def padded_2(block, sides, width):
    for axis, dim in sides:
        count = lax.axis_size(axis)
        forward = [(i, i + 1) for i in range(count - 1)]
        backward = [(target, source) for source, target in forward]
        low = lax.ppermute(
            lax.slice_in_dim(block, block.shape[dim] - width, None, axis=dim), axis, forward
        )
        high = lax.ppermute(lax.slice_in_dim(block, 0, width, axis=dim), axis, backward)
        block = jnp.concatenate([low, block, high], axis=dim)
    return block


def wavenumber(position, length):
    middle = length // 2
    shifted = jnp.where(
        position < middle, position, jnp.where(position == middle, 0, position - length)
    )
    return shifted.astype(jnp.float32) * (2.0 / length)


def to_pencils(spectra):
    count, rows, cols = spectra.shape
    devices = lax.axis_size("row")
    planes = jnp.concatenate([jnp.real(spectra), jnp.imag(spectra)], axis=0).astype(LINK)
    blocks = planes.reshape(2 * count, rows, devices, cols // devices).transpose(2, 0, 1, 3)
    arrived = lax.all_to_all(blocks, "row", split_axis=0, concat_axis=0, tiled=True)
    arrived = arrived.transpose(1, 0, 2, 3).reshape(2 * count, devices * rows, cols // devices)
    arrived = arrived.astype(jnp.float32)
    return lax.complex(arrived[:count], arrived[count:])


def to_rows(spectra):
    count = spectra.shape[0]
    planes = jnp.concatenate([jnp.real(spectra), jnp.imag(spectra)], axis=0).astype(LINK)
    arrived = lax.all_to_all(planes, "row", split_axis=1, concat_axis=2, tiled=True)
    arrived = arrived.astype(jnp.float32)
    return lax.complex(arrived[:count], arrived[count:])


def butterfly_sum(values, axis):
    count = lax.axis_size(axis)
    if count & (count - 1):
        return lax.psum(values, axis)
    index = lax.axis_index(axis)
    stride = 1
    while stride < count:
        radix = 4 if count % (stride * 4) == 0 else 2
        received = [values] + [
            lax.ppermute(values, axis, [(i, i ^ (k * stride)) for i in range(count)])
            for k in range(1, radix)
        ]
        digit = (index // stride) % radix
        ordered = jnp.take(
            jnp.stack(received), jnp.arange(radix, dtype=jnp.int32) ^ digit, axis=0
        )
        values = ordered[0]
        for k in range(1, radix):
            values = values + ordered[k]
        stride *= radix
    return values


def flat_sum(tensors):
    flat = butterfly_sum(jnp.concatenate([t.reshape(-1) for t in tensors]), "row")
    summed = []
    offset = 0
    for t in tensors:
        summed.append(flat[offset : offset + t.size].reshape(t.shape))
        offset += t.size
    return summed


def forward_grid(fields):
    rows = jnp.fft.fft(fields.astype(jnp.complex64), axis=-1)
    return jnp.fft.fft(to_pencils(rows), axis=-2)


def inverse_grid(spectra):
    cols = jnp.fft.ifft(spectra, axis=-2)
    return jnp.fft.ifft(to_rows(cols), axis=-1)


def row_rim(block, depth):
    return padded_2(block, (("row", 1),), depth)


def pad_columns(block):
    return jnp.pad(block, ((0, 0), (0, 0), (1, 1)))


def conv_taps(rows_wide, kernel):
    out_rows = rows_wide.shape[1] - 2
    out_cols = rows_wide.shape[2]
    padded = pad_columns(rows_wide)
    summed = None
    for row_tap in range(3):
        for col_tap in range(3):
            partial_value = jnp.einsum(
                "ci,irx->crx",
                kernel[row_tap, col_tap],
                padded[:, row_tap : row_tap + out_rows, col_tap : col_tap + out_cols],
                preferred_element_type=jnp.float32,
            )
            summed = partial_value if summed is None else summed + partial_value
    return summed


def conv_back(rows_wide, kernel):
    out_rows = rows_wide.shape[1] - 2
    out_cols = rows_wide.shape[2]
    padded = pad_columns(rows_wide)
    summed = None
    for row_tap in range(3):
        for col_tap in range(3):
            partial_value = jnp.einsum(
                "ci,crx->irx",
                kernel[row_tap, col_tap],
                padded[
                    :, 2 - row_tap : 2 - row_tap + out_rows, 2 - col_tap : 2 - col_tap + out_cols
                ],
                preferred_element_type=jnp.float32,
            )
            summed = partial_value if summed is None else summed + partial_value
    return summed


def kernel_grad(upstream, rows_wide):
    out_rows = upstream.shape[1]
    out_cols = upstream.shape[2]
    padded = pad_columns(rows_wide)
    tap_rows = []
    for row_tap in range(3):
        tap_cols = []
        for col_tap in range(3):
            tap_cols.append(
                jnp.einsum(
                    "crx,irx->ci",
                    upstream,
                    padded[:, row_tap : row_tap + out_rows, col_tap : col_tap + out_cols],
                    preferred_element_type=jnp.float32,
                )
            )
        tap_rows.append(jnp.stack(tap_cols))
    return jnp.stack(tap_rows)


def silu_slope(values):
    sigmoid = jax.nn.sigmoid(values)
    return sigmoid * (1.0 + values * (1.0 - sigmoid))


def per_device(
    stokes_q,
    stokes_u,
    wiener_filter,
    inverse_filter,
    lens_norm,
    conv_first,
    bias_first,
    conv_second,
    bias_second,
    head_weight,
    head_bias,
    cotangent,
):
    row_count, col_count = stokes_q.shape
    devices = lax.axis_size("row")
    height = row_count * devices
    pencil = col_count // devices
    band_cols = cotangent.shape[2]
    column_ids = lax.axis_index("row") * pencil + jnp.arange(pencil, dtype=jnp.int32)
    col_freq = wavenumber(column_ids, col_count)[None, :]
    row_freq = wavenumber(jnp.arange(height, dtype=jnp.int32), height)[:, None]
    radius = col_freq * col_freq + row_freq * row_freq
    safe_radius = jnp.where(radius > 0, radius, 1.0)
    cos_twice = (col_freq * col_freq - row_freq * row_freq) / safe_radius
    sin_twice = 2.0 * col_freq * row_freq / safe_radius
    stokes_spec = forward_grid(jnp.stack([stokes_q, stokes_u]))
    emode = cos_twice * stokes_spec[0] + sin_twice * stokes_spec[1]
    wiener_mode = wiener_filter * emode
    packed = inverse_filter * emode - col_freq * wiener_mode
    slope_y = lax.complex(-row_freq * jnp.imag(wiener_mode), row_freq * jnp.real(wiener_mode))
    fields = inverse_grid(jnp.stack([packed, slope_y]))
    filtered = jnp.real(fields[0])
    gradient_x = jnp.imag(fields[0])
    gradient_y = jnp.real(fields[1])
    power = forward_grid(jnp.stack([filtered * gradient_x, filtered * gradient_y]))
    mixed = col_freq * power[0] + row_freq * power[1]
    lens_spec = lax.complex(lens_norm * jnp.imag(mixed), -lens_norm * jnp.real(mixed))
    lens_real = jnp.real(inverse_grid(lens_spec[None])[0])
    band_start = col_count // 2 - band_cols // 2
    band_q = stokes_q[:, band_start : band_start + band_cols]
    band_u = stokes_u[:, band_start : band_start + band_cols]
    stokes_wide = row_rim(jnp.stack([band_q, band_u]).astype(jnp.bfloat16), 3)
    cotangent_wide = row_rim(cotangent, 1)
    lens_band = lens_real[:, band_start : band_start + band_cols]
    lens_wide = row_rim(lens_band.astype(jnp.bfloat16)[None], 3)
    input_wide = jnp.concatenate([lens_wide, stokes_wide], axis=0)
    pre_first = conv_taps(input_wide, conv_first) + bias_first[:, None, None]
    global_rows = lax.axis_index("row") * row_count + jnp.arange(-2, row_count + 2)
    inside = (global_rows >= 0) & (global_rows < height)
    hidden_wide = jnp.where(inside[None, :, None], jax.nn.silu(pre_first), 0.0).astype(
        jnp.bfloat16
    )
    pre_second = conv_taps(hidden_wide, conv_second) + bias_second[:, None, None]
    hidden_second = jax.nn.silu(pre_second[:, 1:-1]).astype(jnp.bfloat16)
    head_out = jnp.einsum(
        "oc,crx->orx", head_weight, hidden_second, preferred_element_type=jnp.float32
    )
    delensed = jnp.stack([band_q, band_u]) + head_out + head_bias[:, None, None]
    grad_head = jnp.einsum(
        "orx,crx->oc", cotangent, hidden_second, preferred_element_type=jnp.float32
    )
    grad_head_bias = jnp.sum(cotangent.astype(jnp.float32), axis=(1, 2))
    through_head = jnp.einsum(
        "oc,orx->crx", head_weight, cotangent_wide, preferred_element_type=jnp.float32
    )
    back_wide = (through_head * silu_slope(pre_second)).astype(jnp.bfloat16)
    back_second = back_wide[:, 1:-1]
    grad_conv_second = kernel_grad(back_second, hidden_wide[:, 1:-1])
    grad_bias_second = jnp.sum(back_second.astype(jnp.float32), axis=(1, 2))
    back_first = (
        conv_back(back_wide, conv_second) * silu_slope(pre_first[:, 2:-2])
    ).astype(jnp.bfloat16)
    grad_conv_first = kernel_grad(back_first, input_wide[:, 2:-2])
    grad_bias_first = jnp.sum(back_first.astype(jnp.float32), axis=(1, 2))
    summed = flat_sum(
        (
            grad_conv_first,
            grad_bias_first,
            grad_conv_second,
            grad_bias_second,
            grad_head,
            grad_head_bias,
        )
    )
    return (delensed, *summed)


def solution(mesh):
    return jax.shard_map(
        per_device,
        mesh=mesh,
        in_specs=(
            P(("patch", "row"), None),
            P(("patch", "row"), None),
            P("patch", "row"),
            P("patch", "row"),
            P("patch", "row"),
            P(),
            P(),
            P(),
            P(),
            P(),
            P(),
            P(None, ("patch", "row"), None),
        ),
        out_specs=(
            P(None, ("patch", "row"), None),
            P("patch", None, None, None),
            P("patch"),
            P("patch", None, None, None),
            P("patch"),
            P("patch", None),
            P("patch"),
        ),
        check_vma=False,
    )
```

```python
import jax
import jax.numpy as jnp
from jax import lax
from jax.sharding import PartitionSpec as P

LINK = jnp.bfloat16


def padded_2(block, sides, width):
    for axis, dim in sides:
        count = lax.axis_size(axis)
        forward = [(i, i + 1) for i in range(count - 1)]
        backward = [(target, source) for source, target in forward]
        low = lax.ppermute(
            lax.slice_in_dim(block, block.shape[dim] - width, None, axis=dim), axis, forward
        )
        high = lax.ppermute(lax.slice_in_dim(block, 0, width, axis=dim), axis, backward)
        block = jnp.concatenate([low, block, high], axis=dim)
    return block


def wavenumber(position, length):
    middle = length // 2
    shifted = jnp.where(
        position < middle, position, jnp.where(position == middle, 0, position - length)
    )
    return shifted.astype(jnp.float32) * (2.0 / length)


def to_pencils(spectra):
    count, rows, cols = spectra.shape
    devices = lax.axis_size("row")
    planes = jnp.concatenate([jnp.real(spectra), jnp.imag(spectra)], axis=0).astype(LINK)
    blocks = planes.reshape(2 * count, rows, devices, cols // devices).transpose(2, 0, 1, 3)
    arrived = lax.all_to_all(blocks, "row", split_axis=0, concat_axis=0, tiled=True)
    arrived = arrived.transpose(1, 0, 2, 3).reshape(2 * count, devices * rows, cols // devices)
    arrived = arrived.astype(jnp.float32)
    return lax.complex(arrived[:count], arrived[count:])


def to_rows(spectra):
    count = spectra.shape[0]
    planes = jnp.concatenate([jnp.real(spectra), jnp.imag(spectra)], axis=0).astype(LINK)
    arrived = lax.all_to_all(planes, "row", split_axis=1, concat_axis=2, tiled=True)
    arrived = arrived.astype(jnp.float32)
    return lax.complex(arrived[:count], arrived[count:])


def butterfly_sum(values, axis):
    count = lax.axis_size(axis)
    if count & (count - 1):
        return lax.psum(values, axis)
    index = lax.axis_index(axis)
    stride = 1
    while stride < count:
        radix = 4 if count % (stride * 4) == 0 else 2
        received = [values] + [
            lax.ppermute(values, axis, [(i, i ^ (k * stride)) for i in range(count)])
            for k in range(1, radix)
        ]
        digit = (index // stride) % radix
        ordered = jnp.take(
            jnp.stack(received), jnp.arange(radix, dtype=jnp.int32) ^ digit, axis=0
        )
        values = ordered[0]
        for k in range(1, radix):
            values = values + ordered[k]
        stride *= radix
    return values


def flat_sum(tensors):
    flat = butterfly_sum(jnp.concatenate([t.reshape(-1) for t in tensors]), "row")
    summed = []
    offset = 0
    for t in tensors:
        summed.append(flat[offset : offset + t.size].reshape(t.shape))
        offset += t.size
    return summed


def forward_grid(fields):
    rows = jnp.fft.fft(fields.astype(jnp.complex64), axis=-1)
    return jnp.fft.fft(to_pencils(rows), axis=-2)


def inverse_grid(spectra):
    cols = jnp.fft.ifft(spectra, axis=-2)
    return jnp.fft.ifft(to_rows(cols), axis=-1)


def row_rim(block, depth):
    return padded_2(block, (("row", 1),), depth)


def pad_columns(block):
    return jnp.pad(block, ((0, 0), (0, 0), (1, 1)))


def conv3(rows_wide, kernel):
    out = lax.conv_general_dilated(
        rows_wide[None],
        kernel,
        window_strides=(1, 1),
        padding=((0, 0), (1, 1)),
        dimension_numbers=("NCHW", "HWOI", "NCHW"),
        preferred_element_type=jnp.float32,
    )
    return out[0]


def conv_taps(rows_wide, kernel):
    out_rows = rows_wide.shape[1] - 2
    out_cols = rows_wide.shape[2]
    padded = pad_columns(rows_wide)
    summed = None
    for row_tap in range(3):
        for col_tap in range(3):
            partial_value = jnp.einsum(
                "ci,irx->crx",
                kernel[row_tap, col_tap],
                padded[:, row_tap : row_tap + out_rows, col_tap : col_tap + out_cols],
                preferred_element_type=jnp.float32,
            )
            summed = partial_value if summed is None else summed + partial_value
    return summed


def conv_back(rows_wide, kernel):
    out_rows = rows_wide.shape[1] - 2
    out_cols = rows_wide.shape[2]
    padded = pad_columns(rows_wide)
    summed = None
    for row_tap in range(3):
        for col_tap in range(3):
            partial_value = jnp.einsum(
                "ci,crx->irx",
                kernel[row_tap, col_tap],
                padded[
                    :, 2 - row_tap : 2 - row_tap + out_rows, 2 - col_tap : 2 - col_tap + out_cols
                ],
                preferred_element_type=jnp.float32,
            )
            summed = partial_value if summed is None else summed + partial_value
    return summed


def kernel_grad(upstream, rows_wide):
    out_rows = upstream.shape[1]
    out_cols = upstream.shape[2]
    padded = pad_columns(rows_wide)
    tap_rows = []
    for row_tap in range(3):
        tap_cols = []
        for col_tap in range(3):
            tap_cols.append(
                jnp.einsum(
                    "crx,irx->ci",
                    upstream,
                    padded[:, row_tap : row_tap + out_rows, col_tap : col_tap + out_cols],
                    preferred_element_type=jnp.float32,
                )
            )
        tap_rows.append(jnp.stack(tap_cols))
    return jnp.stack(tap_rows)


def silu_slope(values):
    sigmoid = jax.nn.sigmoid(values)
    return sigmoid * (1.0 + values * (1.0 - sigmoid))


def per_device(
    stokes_q,
    stokes_u,
    wiener_filter,
    inverse_filter,
    lens_norm,
    conv_first,
    bias_first,
    conv_second,
    bias_second,
    head_weight,
    head_bias,
    cotangent,
):
    row_count, col_count = stokes_q.shape
    devices = lax.axis_size("row")
    height = row_count * devices
    pencil = col_count // devices
    band_cols = cotangent.shape[2]
    column_ids = lax.axis_index("row") * pencil + jnp.arange(pencil, dtype=jnp.int32)
    col_freq = wavenumber(column_ids, col_count)[None, :]
    row_freq = wavenumber(jnp.arange(height, dtype=jnp.int32), height)[:, None]
    radius = col_freq * col_freq + row_freq * row_freq
    safe_radius = jnp.where(radius > 0, radius, 1.0)
    cos_twice = (col_freq * col_freq - row_freq * row_freq) / safe_radius
    sin_twice = 2.0 * col_freq * row_freq / safe_radius
    stokes_spec = forward_grid(jnp.stack([stokes_q, stokes_u]))
    emode = cos_twice * stokes_spec[0] + sin_twice * stokes_spec[1]
    wiener_mode = wiener_filter * emode
    packed = inverse_filter * emode - col_freq * wiener_mode
    slope_y = lax.complex(-row_freq * jnp.imag(wiener_mode), row_freq * jnp.real(wiener_mode))
    fields = inverse_grid(jnp.stack([packed, slope_y]))
    filtered = jnp.real(fields[0])
    gradient_x = jnp.imag(fields[0])
    gradient_y = jnp.real(fields[1])
    power = forward_grid(jnp.stack([filtered * gradient_x, filtered * gradient_y]))
    mixed = col_freq * power[0] + row_freq * power[1]
    lens_spec = lax.complex(lens_norm * jnp.imag(mixed), -lens_norm * jnp.real(mixed))
    lens_real = jnp.real(inverse_grid(lens_spec[None])[0])
    band_start = col_count // 2 - band_cols // 2
    band_q = stokes_q[:, band_start : band_start + band_cols]
    band_u = stokes_u[:, band_start : band_start + band_cols]
    stokes_wide = row_rim(jnp.stack([band_q, band_u]).astype(jnp.bfloat16), 3)
    cotangent_wide = row_rim(cotangent, 1)
    lens_band = lens_real[:, band_start : band_start + band_cols]
    lens_wide = row_rim(lens_band.astype(jnp.bfloat16)[None], 3)
    input_wide = jnp.concatenate([lens_wide, stokes_wide], axis=0)
    pre_first = conv3(input_wide, conv_first) + bias_first[:, None, None]
    global_rows = lax.axis_index("row") * row_count + jnp.arange(-2, row_count + 2)
    inside = (global_rows >= 0) & (global_rows < height)
    hidden_wide = jnp.where(inside[None, :, None], jax.nn.silu(pre_first), 0.0).astype(
        jnp.bfloat16
    )
    pre_second = conv3(hidden_wide, conv_second) + bias_second[:, None, None]
    hidden_second = jax.nn.silu(pre_second[:, 1:-1]).astype(jnp.bfloat16)
    head_out = jnp.einsum(
        "oc,crx->orx", head_weight, hidden_second, preferred_element_type=jnp.float32
    )
    delensed = jnp.stack([band_q, band_u]) + head_out + head_bias[:, None, None]
    grad_head = jnp.einsum(
        "orx,crx->oc", cotangent, hidden_second, preferred_element_type=jnp.float32
    )
    grad_head_bias = jnp.sum(cotangent.astype(jnp.float32), axis=(1, 2))
    through_head = jnp.einsum(
        "oc,orx->crx", head_weight, cotangent_wide, preferred_element_type=jnp.float32
    )
    back_wide = (through_head * silu_slope(pre_second)).astype(jnp.bfloat16)
    back_second = back_wide[:, 1:-1]
    grad_conv_second = kernel_grad(back_second, hidden_wide[:, 1:-1])
    grad_bias_second = jnp.sum(back_second.astype(jnp.float32), axis=(1, 2))
    back_first = (
        conv3(back_wide, jnp.flip(conv_second, (0, 1)).transpose(0, 1, 3, 2))
        * silu_slope(pre_first[:, 2:-2])
    ).astype(jnp.bfloat16)
    grad_conv_first = kernel_grad(back_first, input_wide[:, 2:-2])
    grad_bias_first = jnp.sum(back_first.astype(jnp.float32), axis=(1, 2))
    summed = flat_sum(
        (
            grad_conv_first,
            grad_bias_first,
            grad_conv_second,
            grad_bias_second,
            grad_head,
            grad_head_bias,
        )
    )
    return (delensed, *summed)


def solution(mesh):
    return jax.shard_map(
        per_device,
        mesh=mesh,
        in_specs=(
            P(("patch", "row"), None),
            P(("patch", "row"), None),
            P("patch", "row"),
            P("patch", "row"),
            P("patch", "row"),
            P(),
            P(),
            P(),
            P(),
            P(),
            P(),
            P(None, ("patch", "row"), None),
        ),
        out_specs=(
            P(None, ("patch", "row"), None),
            P("patch", None, None, None),
            P("patch"),
            P("patch", None, None, None),
            P("patch"),
            P("patch", None),
            P("patch"),
        ),
        check_vma=False,
    )
```

```python
import jax
import jax.numpy as jnp
from jax import lax
from jax.sharding import PartitionSpec as P

LINK = jnp.bfloat16


def padded_2(block, sides, width):
    for axis, dim in sides:
        count = lax.axis_size(axis)
        forward = [(i, i + 1) for i in range(count - 1)]
        backward = [(target, source) for source, target in forward]
        low = lax.ppermute(
            lax.slice_in_dim(block, block.shape[dim] - width, None, axis=dim), axis, forward
        )
        high = lax.ppermute(lax.slice_in_dim(block, 0, width, axis=dim), axis, backward)
        block = jnp.concatenate([low, block, high], axis=dim)
    return block


def wavenumber(position, length):
    middle = length // 2
    shifted = jnp.where(
        position < middle, position, jnp.where(position == middle, 0, position - length)
    )
    return shifted.astype(jnp.float32) * (2.0 / length)


def to_pencils(spectra):
    count, rows, cols = spectra.shape
    devices = lax.axis_size("row")
    planes = jnp.concatenate([jnp.real(spectra), jnp.imag(spectra)], axis=0).astype(LINK)
    blocks = planes.reshape(2 * count, rows, devices, cols // devices).transpose(2, 0, 1, 3)
    arrived = lax.all_to_all(blocks, "row", split_axis=0, concat_axis=0, tiled=True)
    arrived = arrived.transpose(1, 0, 2, 3).reshape(2 * count, devices * rows, cols // devices)
    arrived = arrived.astype(jnp.float32)
    return lax.complex(arrived[:count], arrived[count:])


def to_rows(spectra):
    count = spectra.shape[0]
    planes = jnp.concatenate([jnp.real(spectra), jnp.imag(spectra)], axis=0).astype(LINK)
    arrived = lax.all_to_all(planes, "row", split_axis=1, concat_axis=2, tiled=True)
    arrived = arrived.astype(jnp.float32)
    return lax.complex(arrived[:count], arrived[count:])


def butterfly_sum(values, axis):
    count = lax.axis_size(axis)
    if count & (count - 1):
        return lax.psum(values, axis)
    index = lax.axis_index(axis)
    stride = 1
    while stride < count:
        radix = 4 if count % (stride * 4) == 0 else 2
        received = [values] + [
            lax.ppermute(values, axis, [(i, i ^ (k * stride)) for i in range(count)])
            for k in range(1, radix)
        ]
        digit = (index // stride) % radix
        ordered = jnp.take(
            jnp.stack(received), jnp.arange(radix, dtype=jnp.int32) ^ digit, axis=0
        )
        values = ordered[0]
        for k in range(1, radix):
            values = values + ordered[k]
        stride *= radix
    return values


def flat_sum(tensors):
    flat = butterfly_sum(jnp.concatenate([t.reshape(-1) for t in tensors]), "row")
    summed = []
    offset = 0
    for t in tensors:
        summed.append(flat[offset : offset + t.size].reshape(t.shape))
        offset += t.size
    return summed


def forward_grid(fields):
    packed = jnp.fft.fft(lax.complex(fields[0], fields[1]), axis=-1)
    mirrored = jnp.conj(jnp.roll(jnp.flip(packed, axis=-1), 1, axis=-1))
    rows = jnp.stack([0.5 * (packed + mirrored), -0.5j * (packed - mirrored)])
    return jnp.fft.fft(to_pencils(rows), axis=-2)


def inverse_grid(spectra):
    cols = jnp.fft.ifft(spectra, axis=-2)
    return jnp.fft.ifft(to_rows(cols), axis=-1)


def row_rim(block, depth):
    return padded_2(block, (("row", 1),), depth)


def pad_columns(block):
    return jnp.pad(block, ((0, 0), (0, 0), (1, 1)))


def conv_taps(rows_wide, kernel):
    out_rows = rows_wide.shape[1] - 2
    out_cols = rows_wide.shape[2]
    padded = pad_columns(rows_wide)
    summed = None
    for row_tap in range(3):
        for col_tap in range(3):
            partial_value = jnp.einsum(
                "ci,irx->crx",
                kernel[row_tap, col_tap],
                padded[:, row_tap : row_tap + out_rows, col_tap : col_tap + out_cols],
                preferred_element_type=jnp.float32,
            )
            summed = partial_value if summed is None else summed + partial_value
    return summed


def conv_back(rows_wide, kernel):
    out_rows = rows_wide.shape[1] - 2
    out_cols = rows_wide.shape[2]
    padded = pad_columns(rows_wide)
    summed = None
    for row_tap in range(3):
        for col_tap in range(3):
            partial_value = jnp.einsum(
                "ci,crx->irx",
                kernel[row_tap, col_tap],
                padded[
                    :, 2 - row_tap : 2 - row_tap + out_rows, 2 - col_tap : 2 - col_tap + out_cols
                ],
                preferred_element_type=jnp.float32,
            )
            summed = partial_value if summed is None else summed + partial_value
    return summed


def kernel_grad(upstream, rows_wide):
    out_rows = upstream.shape[1]
    out_cols = upstream.shape[2]
    padded = pad_columns(rows_wide)
    tap_rows = []
    for row_tap in range(3):
        tap_cols = []
        for col_tap in range(3):
            tap_cols.append(
                jnp.einsum(
                    "crx,irx->ci",
                    upstream,
                    padded[:, row_tap : row_tap + out_rows, col_tap : col_tap + out_cols],
                    preferred_element_type=jnp.float32,
                )
            )
        tap_rows.append(jnp.stack(tap_cols))
    return jnp.stack(tap_rows)


def silu_slope(values):
    sigmoid = jax.nn.sigmoid(values)
    return sigmoid * (1.0 + values * (1.0 - sigmoid))


def per_device(
    stokes_q,
    stokes_u,
    wiener_filter,
    inverse_filter,
    lens_norm,
    conv_first,
    bias_first,
    conv_second,
    bias_second,
    head_weight,
    head_bias,
    cotangent,
):
    row_count, col_count = stokes_q.shape
    devices = lax.axis_size("row")
    height = row_count * devices
    pencil = col_count // devices
    band_cols = cotangent.shape[2]
    column_ids = lax.axis_index("row") * pencil + jnp.arange(pencil, dtype=jnp.int32)
    col_freq = wavenumber(column_ids, col_count)[None, :]
    row_freq = wavenumber(jnp.arange(height, dtype=jnp.int32), height)[:, None]
    radius = col_freq * col_freq + row_freq * row_freq
    safe_radius = jnp.where(radius > 0, radius, 1.0)
    cos_twice = (col_freq * col_freq - row_freq * row_freq) / safe_radius
    sin_twice = 2.0 * col_freq * row_freq / safe_radius
    stokes_spec = forward_grid(jnp.stack([stokes_q, stokes_u]))
    emode = cos_twice * stokes_spec[0] + sin_twice * stokes_spec[1]
    wiener_mode = wiener_filter * emode
    packed = inverse_filter * emode - col_freq * wiener_mode
    slope_y = lax.complex(-row_freq * jnp.imag(wiener_mode), row_freq * jnp.real(wiener_mode))
    fields = inverse_grid(jnp.stack([packed, slope_y]))
    filtered = jnp.real(fields[0])
    gradient_x = jnp.imag(fields[0])
    gradient_y = jnp.real(fields[1])
    power = forward_grid(jnp.stack([filtered * gradient_x, filtered * gradient_y]))
    mixed = col_freq * power[0] + row_freq * power[1]
    lens_spec = lax.complex(lens_norm * jnp.imag(mixed), -lens_norm * jnp.real(mixed))
    lens_real = jnp.real(inverse_grid(lens_spec[None])[0])
    band_start = col_count // 2 - band_cols // 2
    band_q = stokes_q[:, band_start : band_start + band_cols]
    band_u = stokes_u[:, band_start : band_start + band_cols]
    stokes_wide = row_rim(jnp.stack([band_q, band_u]).astype(jnp.bfloat16), 3)
    cotangent_wide = row_rim(cotangent, 1)
    lens_band = lens_real[:, band_start : band_start + band_cols]
    lens_wide = row_rim(lens_band.astype(jnp.bfloat16)[None], 3)
    input_wide = jnp.concatenate([lens_wide, stokes_wide], axis=0)
    pre_first = conv_taps(input_wide, conv_first) + bias_first[:, None, None]
    global_rows = lax.axis_index("row") * row_count + jnp.arange(-2, row_count + 2)
    inside = (global_rows >= 0) & (global_rows < height)
    hidden_wide = jnp.where(inside[None, :, None], jax.nn.silu(pre_first), 0.0).astype(
        jnp.bfloat16
    )
    pre_second = conv_taps(hidden_wide, conv_second) + bias_second[:, None, None]
    hidden_second = jax.nn.silu(pre_second[:, 1:-1]).astype(jnp.bfloat16)
    head_out = jnp.einsum(
        "oc,crx->orx", head_weight, hidden_second, preferred_element_type=jnp.float32
    )
    delensed = jnp.stack([band_q, band_u]) + head_out + head_bias[:, None, None]
    grad_head = jnp.einsum(
        "orx,crx->oc", cotangent, hidden_second, preferred_element_type=jnp.float32
    )
    grad_head_bias = jnp.sum(cotangent.astype(jnp.float32), axis=(1, 2))
    through_head = jnp.einsum(
        "oc,orx->crx", head_weight, cotangent_wide, preferred_element_type=jnp.float32
    )
    back_wide = (through_head * silu_slope(pre_second)).astype(jnp.bfloat16)
    back_second = back_wide[:, 1:-1]
    grad_conv_second = kernel_grad(back_second, hidden_wide[:, 1:-1])
    grad_bias_second = jnp.sum(back_second.astype(jnp.float32), axis=(1, 2))
    back_first = (
        conv_back(back_wide, conv_second) * silu_slope(pre_first[:, 2:-2])
    ).astype(jnp.bfloat16)
    grad_conv_first = kernel_grad(back_first, input_wide[:, 2:-2])
    grad_bias_first = jnp.sum(back_first.astype(jnp.float32), axis=(1, 2))
    summed = flat_sum(
        (
            grad_conv_first,
            grad_bias_first,
            grad_conv_second,
            grad_bias_second,
            grad_head,
            grad_head_bias,
        )
    )
    return (delensed, *summed)


def solution(mesh):
    return jax.shard_map(
        per_device,
        mesh=mesh,
        in_specs=(
            P(("patch", "row"), None),
            P(("patch", "row"), None),
            P("patch", "row"),
            P("patch", "row"),
            P("patch", "row"),
            P(),
            P(),
            P(),
            P(),
            P(),
            P(),
            P(None, ("patch", "row"), None),
        ),
        out_specs=(
            P(None, ("patch", "row"), None),
            P("patch", None, None, None),
            P("patch"),
            P("patch", None, None, None),
            P("patch"),
            P("patch", None),
            P("patch"),
        ),
        check_vma=False,
    )
```

```python
import jax
import jax.numpy as jnp
from jax import lax
from jax.sharding import PartitionSpec as P

LINK = jnp.bfloat16


def padded_2(block, sides, width):
    for axis, dim in sides:
        count = lax.axis_size(axis)
        forward = [(i, i + 1) for i in range(count - 1)]
        backward = [(target, source) for source, target in forward]
        low = lax.ppermute(
            lax.slice_in_dim(block, block.shape[dim] - width, None, axis=dim), axis, forward
        )
        high = lax.ppermute(lax.slice_in_dim(block, 0, width, axis=dim), axis, backward)
        block = jnp.concatenate([low, block, high], axis=dim)
    return block


def wavenumber(position, length):
    middle = length // 2
    shifted = jnp.where(
        position < middle, position, jnp.where(position == middle, 0, position - length)
    )
    return shifted.astype(jnp.float32) * (2.0 / length)


def to_pencils(spectra):
    count, rows, cols = spectra.shape
    devices = lax.axis_size("row")
    planes = jnp.concatenate([jnp.real(spectra), jnp.imag(spectra)], axis=0).astype(LINK)
    blocks = planes.reshape(2 * count, rows, devices, cols // devices).transpose(2, 0, 1, 3)
    arrived = lax.all_to_all(blocks, "row", split_axis=0, concat_axis=0, tiled=True)
    arrived = arrived.transpose(1, 0, 2, 3).reshape(2 * count, devices * rows, cols // devices)
    arrived = arrived.astype(jnp.float32)
    return lax.complex(arrived[:count], arrived[count:])


def to_rows(spectra):
    count = spectra.shape[0]
    planes = jnp.concatenate([jnp.real(spectra), jnp.imag(spectra)], axis=0).astype(LINK)
    arrived = lax.all_to_all(planes, "row", split_axis=1, concat_axis=2, tiled=True)
    arrived = arrived.astype(jnp.float32)
    return lax.complex(arrived[:count], arrived[count:])


def butterfly_sum(values, axis):
    count = lax.axis_size(axis)
    if count & (count - 1):
        return lax.psum(values, axis)
    index = lax.axis_index(axis)
    stride = 1
    while stride < count:
        radix = 4 if count % (stride * 4) == 0 else 2
        received = [values] + [
            lax.ppermute(values, axis, [(i, i ^ (k * stride)) for i in range(count)])
            for k in range(1, radix)
        ]
        digit = (index // stride) % radix
        ordered = jnp.take(
            jnp.stack(received), jnp.arange(radix, dtype=jnp.int32) ^ digit, axis=0
        )
        values = ordered[0]
        for k in range(1, radix):
            values = values + ordered[k]
        stride *= radix
    return values


def flat_sum(tensors):
    flat = butterfly_sum(jnp.concatenate([t.reshape(-1) for t in tensors]), "row")
    summed = []
    offset = 0
    for t in tensors:
        summed.append(flat[offset : offset + t.size].reshape(t.shape))
        offset += t.size
    return summed


def forward_grid(fields):
    rows = jnp.fft.fft(fields.astype(jnp.complex64), axis=-1)
    return jnp.fft.fft(to_pencils(rows), axis=-2)


def inverse_grid(spectra):
    cols = jnp.fft.ifft(spectra, axis=-2)
    return jnp.fft.ifft(to_rows(cols), axis=-1)


def row_rim(block, depth):
    return padded_2(block, (("row", 1),), depth)


def pad_columns(block):
    return jnp.pad(block, ((0, 0), (0, 0), (1, 1)))


def conv_taps(rows_wide, kernel):
    out_rows = rows_wide.shape[1] - 2
    out_cols = rows_wide.shape[2]
    padded = pad_columns(rows_wide)
    summed = None
    for row_tap in range(3):
        for col_tap in range(3):
            partial_value = jnp.einsum(
                "ci,irx->crx",
                kernel[row_tap, col_tap],
                padded[:, row_tap : row_tap + out_rows, col_tap : col_tap + out_cols],
                preferred_element_type=jnp.float32,
            )
            summed = partial_value if summed is None else summed + partial_value
    return summed


def conv_back(rows_wide, kernel):
    out_rows = rows_wide.shape[1] - 2
    out_cols = rows_wide.shape[2]
    padded = pad_columns(rows_wide)
    summed = None
    for row_tap in range(3):
        for col_tap in range(3):
            partial_value = jnp.einsum(
                "ci,crx->irx",
                kernel[row_tap, col_tap],
                padded[
                    :, 2 - row_tap : 2 - row_tap + out_rows, 2 - col_tap : 2 - col_tap + out_cols
                ],
                preferred_element_type=jnp.float32,
            )
            summed = partial_value if summed is None else summed + partial_value
    return summed


def kernel_grad(upstream, rows_wide):
    out_rows = upstream.shape[1]
    out_cols = upstream.shape[2]
    padded = pad_columns(rows_wide)
    tap_rows = []
    for row_tap in range(3):
        tap_cols = []
        for col_tap in range(3):
            tap_cols.append(
                jnp.einsum(
                    "crx,irx->ci",
                    upstream,
                    padded[:, row_tap : row_tap + out_rows, col_tap : col_tap + out_cols],
                    preferred_element_type=jnp.float32,
                )
            )
        tap_rows.append(jnp.stack(tap_cols))
    return jnp.stack(tap_rows)


def silu_slope(values):
    sigmoid = jax.nn.sigmoid(values)
    return sigmoid * (1.0 + values * (1.0 - sigmoid))


def per_device(
    stokes_q,
    stokes_u,
    wiener_filter,
    inverse_filter,
    lens_norm,
    conv_first,
    bias_first,
    conv_second,
    bias_second,
    head_weight,
    head_bias,
    cotangent,
):
    row_count, col_count = stokes_q.shape
    devices = lax.axis_size("row")
    height = row_count * devices
    pencil = col_count // devices
    band_cols = cotangent.shape[2]
    column_ids = lax.axis_index("row") * pencil + jnp.arange(pencil, dtype=jnp.int32)
    col_freq = wavenumber(column_ids, col_count)[None, :]
    row_freq = wavenumber(jnp.arange(height, dtype=jnp.int32), height)[:, None]
    radius = col_freq * col_freq + row_freq * row_freq
    safe_radius = jnp.where(radius > 0, radius, 1.0)
    cos_twice = (col_freq * col_freq - row_freq * row_freq) / safe_radius
    sin_twice = 2.0 * col_freq * row_freq / safe_radius
    stokes_spec = forward_grid(jnp.stack([stokes_q, stokes_u]))
    emode = cos_twice * stokes_spec[0] + sin_twice * stokes_spec[1]
    wiener_mode = wiener_filter * emode
    packed = inverse_filter * emode - col_freq * wiener_mode
    slope_y = lax.complex(-row_freq * jnp.imag(wiener_mode), row_freq * jnp.real(wiener_mode))
    fields = inverse_grid(jnp.stack([packed, slope_y]))
    filtered = jnp.real(fields[0])
    gradient_x = jnp.imag(fields[0])
    gradient_y = jnp.real(fields[1])
    power = forward_grid(jnp.stack([filtered * gradient_x, filtered * gradient_y]))
    mixed = col_freq * power[0] + row_freq * power[1]
    lens_spec = lax.complex(lens_norm * jnp.imag(mixed), -lens_norm * jnp.real(mixed))
    lens_real = jnp.real(inverse_grid(lens_spec[None])[0])
    band_start = col_count // 2 - band_cols // 2
    band_q = stokes_q[:, band_start : band_start + band_cols]
    band_u = stokes_u[:, band_start : band_start + band_cols]
    stokes_wide = row_rim(jnp.stack([band_q, band_u]).astype(jnp.bfloat16), 3)
    cotangent_wide = row_rim(cotangent, 1)
    lens_band = lens_real[:, band_start : band_start + band_cols]
    lens_wide = row_rim(lens_band.astype(jnp.bfloat16)[None], 3)
    input_wide = jnp.concatenate([lens_wide, stokes_wide], axis=0)
    pre_first = conv_taps(input_wide, conv_first) + bias_first[:, None, None]
    global_rows = lax.axis_index("row") * row_count + jnp.arange(-2, row_count + 2)
    inside = (global_rows >= 0) & (global_rows < height)
    hidden_wide = jnp.where(inside[None, :, None], jax.nn.silu(pre_first), 0.0).astype(
        jnp.bfloat16
    )
    pre_second = conv_taps(hidden_wide, conv_second) + bias_second[:, None, None]
    hidden_second = jax.nn.silu(pre_second[:, 1:-1]).astype(jnp.bfloat16)
    head_out = jnp.einsum(
        "oc,crx->orx", head_weight, hidden_second, preferred_element_type=jnp.float32
    )
    delensed = jnp.stack([band_q, band_u]) + head_out + head_bias[:, None, None]
    grad_head = jnp.einsum(
        "orx,crx->oc", cotangent, hidden_second, preferred_element_type=jnp.float32
    )
    grad_head_bias = jnp.sum(cotangent.astype(jnp.float32), axis=(1, 2))
    through_head = jnp.einsum(
        "oc,orx->crx", head_weight, cotangent_wide, preferred_element_type=jnp.float32
    )
    back_wide = (through_head * silu_slope(pre_second)).astype(jnp.bfloat16)
    back_second = back_wide[:, 1:-1]
    grad_conv_second = kernel_grad(back_second, hidden_wide[:, 1:-1])
    grad_bias_second = jnp.sum(back_second.astype(jnp.float32), axis=(1, 2))
    back_first = (
        conv_back(back_wide, conv_second) * silu_slope(pre_first[:, 2:-2])
    ).astype(jnp.bfloat16)
    grad_conv_first = kernel_grad(back_first, input_wide[:, 2:-2])
    grad_bias_first = jnp.sum(back_first.astype(jnp.float32), axis=(1, 2))
    summed = flat_sum(
        (
            grad_conv_second,
            grad_conv_first,
            grad_bias_first,
            grad_bias_second,
            grad_head,
            grad_head_bias,
        )
    )
    return (delensed, summed[1], summed[2], summed[0], *summed[3:])


def solution(mesh):
    return jax.shard_map(
        per_device,
        mesh=mesh,
        in_specs=(
            P(("patch", "row"), None),
            P(("patch", "row"), None),
            P("patch", "row"),
            P("patch", "row"),
            P("patch", "row"),
            P(),
            P(),
            P(),
            P(),
            P(),
            P(),
            P(None, ("patch", "row"), None),
        ),
        out_specs=(
            P(None, ("patch", "row"), None),
            P("patch", None, None, None),
            P("patch"),
            P("patch", None, None, None),
            P("patch"),
            P("patch", None),
            P("patch"),
        ),
        check_vma=False,
    )
```

```python
import jax
import jax.numpy as jnp
from jax import lax
from jax.sharding import PartitionSpec as P

LINK = jnp.bfloat16


def padded_2(block, sides, width):
    for axis, dim in sides:
        count = lax.axis_size(axis)
        forward = [(i, i + 1) for i in range(count - 1)]
        backward = [(target, source) for source, target in forward]
        low = lax.ppermute(
            lax.slice_in_dim(block, block.shape[dim] - width, None, axis=dim), axis, forward
        )
        high = lax.ppermute(lax.slice_in_dim(block, 0, width, axis=dim), axis, backward)
        block = jnp.concatenate([low, block, high], axis=dim)
    return block


def wavenumber(position, length):
    middle = length // 2
    shifted = jnp.where(
        position < middle, position, jnp.where(position == middle, 0, position - length)
    )
    return shifted.astype(jnp.float32) * (2.0 / length)


def to_pencils(spectra):
    count, rows, cols = spectra.shape
    devices = lax.axis_size("row")
    planes = jnp.concatenate([jnp.real(spectra), jnp.imag(spectra)], axis=0).astype(LINK)
    blocks = planes.reshape(2 * count, rows, devices, cols // devices).transpose(2, 0, 1, 3)
    arrived = lax.all_to_all(blocks, "row", split_axis=0, concat_axis=0, tiled=True)
    arrived = arrived.transpose(1, 0, 2, 3).reshape(2 * count, devices * rows, cols // devices)
    arrived = arrived.astype(jnp.float32)
    return lax.complex(arrived[:count], arrived[count:])


def to_rows(spectra):
    count = spectra.shape[0]
    planes = jnp.concatenate([jnp.real(spectra), jnp.imag(spectra)], axis=0).astype(LINK)
    arrived = lax.all_to_all(planes, "row", split_axis=1, concat_axis=2, tiled=True)
    arrived = arrived.astype(jnp.float32)
    return lax.complex(arrived[:count], arrived[count:])


def butterfly_sum(values, axis):
    count = lax.axis_size(axis)
    if count & (count - 1):
        return lax.psum(values, axis)
    index = lax.axis_index(axis)
    stride = 1
    while stride < count:
        radix = 4 if count % (stride * 4) == 0 else 2
        received = [values] + [
            lax.ppermute(values, axis, [(i, i ^ (k * stride)) for i in range(count)])
            for k in range(1, radix)
        ]
        digit = (index // stride) % radix
        ordered = jnp.take(
            jnp.stack(received), jnp.arange(radix, dtype=jnp.int32) ^ digit, axis=0
        )
        values = ordered[0]
        for k in range(1, radix):
            values = values + ordered[k]
        stride *= radix
    return values


def flat_sum(tensors):
    flat = butterfly_sum(jnp.concatenate([t.reshape(-1) for t in tensors]), "row")
    summed = []
    offset = 0
    for t in tensors:
        summed.append(flat[offset : offset + t.size].reshape(t.shape))
        offset += t.size
    return summed


def forward_grid(fields):
    rows = jnp.fft.fft(fields.astype(jnp.complex64), axis=-1)
    return jnp.fft.fft(to_pencils(rows), axis=-2)


def inverse_grid(spectra):
    cols = jnp.fft.ifft(spectra, axis=-2)
    return jnp.fft.ifft(to_rows(cols), axis=-1)


def row_rim(block, depth):
    return padded_2(block, (("row", 1),), depth)


def pad_columns(block):
    return jnp.pad(block, ((0, 0), (0, 0), (1, 1)))


def tap_stack(rows_wide):
    out_rows = rows_wide.shape[1] - 2
    out_cols = rows_wide.shape[2]
    padded = pad_columns(rows_wide)
    return jnp.concatenate(
        [
            padded[:, row_tap : row_tap + out_rows, col_tap : col_tap + out_cols]
            for row_tap in range(3)
            for col_tap in range(3)
        ],
        axis=0,
    )


def conv_taps(rows_wide, kernel):
    out_rows = rows_wide.shape[1] - 2
    out_cols = rows_wide.shape[2]
    padded = pad_columns(rows_wide)
    summed = None
    for row_tap in range(3):
        for col_tap in range(3):
            partial_value = jnp.einsum(
                "ci,irx->crx",
                kernel[row_tap, col_tap],
                padded[:, row_tap : row_tap + out_rows, col_tap : col_tap + out_cols],
                preferred_element_type=jnp.float32,
            )
            summed = partial_value if summed is None else summed + partial_value
    return summed


def conv_back(rows_wide, kernel):
    out_rows = rows_wide.shape[1] - 2
    out_cols = rows_wide.shape[2]
    padded = pad_columns(rows_wide)
    summed = None
    for row_tap in range(3):
        for col_tap in range(3):
            partial_value = jnp.einsum(
                "ci,crx->irx",
                kernel[row_tap, col_tap],
                padded[
                    :, 2 - row_tap : 2 - row_tap + out_rows, 2 - col_tap : 2 - col_tap + out_cols
                ],
                preferred_element_type=jnp.float32,
            )
            summed = partial_value if summed is None else summed + partial_value
    return summed


def kernel_grad(upstream, rows_wide):
    out_rows = upstream.shape[1]
    out_cols = upstream.shape[2]
    padded = pad_columns(rows_wide)
    tap_rows = []
    for row_tap in range(3):
        tap_cols = []
        for col_tap in range(3):
            tap_cols.append(
                jnp.einsum(
                    "crx,irx->ci",
                    upstream,
                    padded[:, row_tap : row_tap + out_rows, col_tap : col_tap + out_cols],
                    preferred_element_type=jnp.float32,
                )
            )
        tap_rows.append(jnp.stack(tap_cols))
    return jnp.stack(tap_rows)


def silu_slope(values):
    sigmoid = jax.nn.sigmoid(values)
    return sigmoid * (1.0 + values * (1.0 - sigmoid))


def per_device(
    stokes_q,
    stokes_u,
    wiener_filter,
    inverse_filter,
    lens_norm,
    conv_first,
    bias_first,
    conv_second,
    bias_second,
    head_weight,
    head_bias,
    cotangent,
):
    row_count, col_count = stokes_q.shape
    devices = lax.axis_size("row")
    height = row_count * devices
    pencil = col_count // devices
    band_cols = cotangent.shape[2]
    column_ids = lax.axis_index("row") * pencil + jnp.arange(pencil, dtype=jnp.int32)
    col_freq = wavenumber(column_ids, col_count)[None, :]
    row_freq = wavenumber(jnp.arange(height, dtype=jnp.int32), height)[:, None]
    radius = col_freq * col_freq + row_freq * row_freq
    safe_radius = jnp.where(radius > 0, radius, 1.0)
    cos_twice = (col_freq * col_freq - row_freq * row_freq) / safe_radius
    sin_twice = 2.0 * col_freq * row_freq / safe_radius
    stokes_spec = forward_grid(jnp.stack([stokes_q, stokes_u]))
    emode = cos_twice * stokes_spec[0] + sin_twice * stokes_spec[1]
    wiener_mode = wiener_filter * emode
    packed = inverse_filter * emode - col_freq * wiener_mode
    slope_y = lax.complex(-row_freq * jnp.imag(wiener_mode), row_freq * jnp.real(wiener_mode))
    fields = inverse_grid(jnp.stack([packed, slope_y]))
    filtered = jnp.real(fields[0])
    gradient_x = jnp.imag(fields[0])
    gradient_y = jnp.real(fields[1])
    power = forward_grid(jnp.stack([filtered * gradient_x, filtered * gradient_y]))
    mixed = col_freq * power[0] + row_freq * power[1]
    lens_spec = lax.complex(lens_norm * jnp.imag(mixed), -lens_norm * jnp.real(mixed))
    lens_real = jnp.real(inverse_grid(lens_spec[None])[0])
    band_start = col_count // 2 - band_cols // 2
    band_q = stokes_q[:, band_start : band_start + band_cols]
    band_u = stokes_u[:, band_start : band_start + band_cols]
    stokes_wide = row_rim(jnp.stack([band_q, band_u]).astype(jnp.bfloat16), 3)
    cotangent_wide = row_rim(cotangent, 1)
    lens_band = lens_real[:, band_start : band_start + band_cols]
    lens_wide = row_rim(lens_band.astype(jnp.bfloat16)[None], 3)
    input_wide = jnp.concatenate([lens_wide, stokes_wide], axis=0)
    input_taps = tap_stack(input_wide)
    first_matrix = conv_first.transpose(2, 0, 1, 3).reshape(conv_first.shape[2], -1)
    pre_first = (
        jnp.einsum(
            "ck,krx->crx", first_matrix, input_taps, preferred_element_type=jnp.float32
        )
        + bias_first[:, None, None]
    )
    global_rows = lax.axis_index("row") * row_count + jnp.arange(-2, row_count + 2)
    inside = (global_rows >= 0) & (global_rows < height)
    hidden_wide = jnp.where(inside[None, :, None], jax.nn.silu(pre_first), 0.0).astype(
        jnp.bfloat16
    )
    pre_second = conv_taps(hidden_wide, conv_second) + bias_second[:, None, None]
    hidden_second = jax.nn.silu(pre_second[:, 1:-1]).astype(jnp.bfloat16)
    head_out = jnp.einsum(
        "oc,crx->orx", head_weight, hidden_second, preferred_element_type=jnp.float32
    )
    delensed = jnp.stack([band_q, band_u]) + head_out + head_bias[:, None, None]
    grad_head = jnp.einsum(
        "orx,crx->oc", cotangent, hidden_second, preferred_element_type=jnp.float32
    )
    grad_head_bias = jnp.sum(cotangent.astype(jnp.float32), axis=(1, 2))
    through_head = jnp.einsum(
        "oc,orx->crx", head_weight, cotangent_wide, preferred_element_type=jnp.float32
    )
    back_wide = (through_head * silu_slope(pre_second)).astype(jnp.bfloat16)
    back_second = back_wide[:, 1:-1]
    grad_conv_second = kernel_grad(back_second, hidden_wide[:, 1:-1])
    grad_bias_second = jnp.sum(back_second.astype(jnp.float32), axis=(1, 2))
    back_first = (
        conv_back(back_wide, conv_second) * silu_slope(pre_first[:, 2:-2])
    ).astype(jnp.bfloat16)
    first_grad = jnp.einsum(
        "crx,krx->ck",
        back_first,
        input_taps[:, 2 : 2 + row_count],
        preferred_element_type=jnp.float32,
    )
    grad_conv_first = first_grad.reshape(conv_first.shape[2], 3, 3, -1).transpose(1, 2, 0, 3)
    grad_bias_first = jnp.sum(back_first.astype(jnp.float32), axis=(1, 2))
    summed = flat_sum(
        (
            grad_conv_second,
            grad_conv_first,
            grad_bias_first,
            grad_bias_second,
            grad_head,
            grad_head_bias,
        )
    )
    return (delensed, summed[1], summed[2], summed[0], *summed[3:])


def solution(mesh):
    return jax.shard_map(
        per_device,
        mesh=mesh,
        in_specs=(
            P(("patch", "row"), None),
            P(("patch", "row"), None),
            P("patch", "row"),
            P("patch", "row"),
            P("patch", "row"),
            P(),
            P(),
            P(),
            P(),
            P(),
            P(),
            P(None, ("patch", "row"), None),
        ),
        out_specs=(
            P(None, ("patch", "row"), None),
            P("patch", None, None, None),
            P("patch"),
            P("patch", None, None, None),
            P("patch"),
            P("patch", None),
            P("patch"),
        ),
        check_vma=False,
    )
```

```python
import jax
import jax.numpy as jnp
from jax import lax
from jax.sharding import PartitionSpec as P

LINK = jnp.bfloat16


def padded_2(block, sides, width):
    for axis, dim in sides:
        count = lax.axis_size(axis)
        forward = [(i, i + 1) for i in range(count - 1)]
        backward = [(target, source) for source, target in forward]
        low = lax.ppermute(
            lax.slice_in_dim(block, block.shape[dim] - width, None, axis=dim), axis, forward
        )
        high = lax.ppermute(lax.slice_in_dim(block, 0, width, axis=dim), axis, backward)
        block = jnp.concatenate([low, block, high], axis=dim)
    return block


def wavenumber(position, length):
    middle = length // 2
    shifted = jnp.where(
        position < middle, position, jnp.where(position == middle, 0, position - length)
    )
    return shifted.astype(jnp.float32) * (2.0 / length)


def to_pencils(spectra):
    count, rows, cols = spectra.shape
    devices = lax.axis_size("row")
    planes = jnp.concatenate([jnp.real(spectra), jnp.imag(spectra)], axis=0).astype(LINK)
    blocks = planes.reshape(2 * count, rows, devices, cols // devices).transpose(2, 0, 1, 3)
    arrived = lax.all_to_all(blocks, "row", split_axis=0, concat_axis=0, tiled=True)
    arrived = arrived.transpose(1, 0, 2, 3).reshape(2 * count, devices * rows, cols // devices)
    arrived = arrived.astype(jnp.float32)
    return lax.complex(arrived[:count], arrived[count:])


def to_rows(spectra):
    count = spectra.shape[0]
    planes = jnp.concatenate([jnp.real(spectra), jnp.imag(spectra)], axis=0).astype(LINK)
    arrived = lax.all_to_all(planes, "row", split_axis=1, concat_axis=2, tiled=True)
    arrived = arrived.astype(jnp.float32)
    return lax.complex(arrived[:count], arrived[count:])


def butterfly_sum(values, axis):
    count = lax.axis_size(axis)
    if count & (count - 1):
        return lax.psum(values, axis)
    index = lax.axis_index(axis)
    stride = 1
    while stride < count:
        radix = 4 if count % (stride * 4) == 0 else 2
        received = [values] + [
            lax.ppermute(values, axis, [(i, i ^ (k * stride)) for i in range(count)])
            for k in range(1, radix)
        ]
        digit = (index // stride) % radix
        ordered = jnp.take(
            jnp.stack(received), jnp.arange(radix, dtype=jnp.int32) ^ digit, axis=0
        )
        values = ordered[0]
        for k in range(1, radix):
            values = values + ordered[k]
        stride *= radix
    return values


def exchange_sum(values, axis):
    count = lax.axis_size(axis)
    size = values.shape[0]
    chunk = -(-size // count)
    blocks = jnp.pad(values, (0, chunk * count - size)).reshape(count, chunk)
    gathered = lax.all_to_all(blocks, axis, 0, 0, tiled=True)
    part = gathered[0]
    for k in range(1, count):
        part = part + gathered[k]
    spread = jnp.broadcast_to(part[None], (count, chunk))
    summed = lax.all_to_all(spread, axis, 0, 0, tiled=True)
    return summed.reshape(-1)[:size]


def flat_sum(tensors):
    flat = exchange_sum(jnp.concatenate([t.reshape(-1) for t in tensors]), "row")
    summed = []
    offset = 0
    for t in tensors:
        summed.append(flat[offset : offset + t.size].reshape(t.shape))
        offset += t.size
    return summed


def forward_grid(fields):
    rows = jnp.fft.fft(fields.astype(jnp.complex64), axis=-1)
    return jnp.fft.fft(to_pencils(rows), axis=-2)


def inverse_grid(spectra):
    cols = jnp.fft.ifft(spectra, axis=-2)
    return jnp.fft.ifft(to_rows(cols), axis=-1)


def row_rim(block, depth):
    return padded_2(block, (("row", 1),), depth)


def pad_columns(block):
    return jnp.pad(block, ((0, 0), (0, 0), (1, 1)))


def tap_stack(rows_wide):
    out_rows = rows_wide.shape[1] - 2
    out_cols = rows_wide.shape[2]
    padded = pad_columns(rows_wide)
    return jnp.concatenate(
        [
            padded[:, row_tap : row_tap + out_rows, col_tap : col_tap + out_cols]
            for row_tap in range(3)
            for col_tap in range(3)
        ],
        axis=0,
    )


def conv_taps(rows_wide, kernel):
    out_rows = rows_wide.shape[1] - 2
    out_cols = rows_wide.shape[2]
    padded = pad_columns(rows_wide)
    summed = None
    for row_tap in range(3):
        for col_tap in range(3):
            partial_value = jnp.einsum(
                "ci,irx->crx",
                kernel[row_tap, col_tap],
                padded[:, row_tap : row_tap + out_rows, col_tap : col_tap + out_cols],
                preferred_element_type=jnp.float32,
            )
            summed = partial_value if summed is None else summed + partial_value
    return summed


def conv_back(rows_wide, kernel):
    out_rows = rows_wide.shape[1] - 2
    out_cols = rows_wide.shape[2]
    padded = pad_columns(rows_wide)
    summed = None
    for row_tap in range(3):
        for col_tap in range(3):
            partial_value = jnp.einsum(
                "ci,crx->irx",
                kernel[row_tap, col_tap],
                padded[
                    :, 2 - row_tap : 2 - row_tap + out_rows, 2 - col_tap : 2 - col_tap + out_cols
                ],
                preferred_element_type=jnp.float32,
            )
            summed = partial_value if summed is None else summed + partial_value
    return summed


def kernel_grad(upstream, rows_wide):
    out_rows = upstream.shape[1]
    out_cols = upstream.shape[2]
    padded = pad_columns(rows_wide)
    tap_rows = []
    for row_tap in range(3):
        tap_cols = []
        for col_tap in range(3):
            tap_cols.append(
                jnp.einsum(
                    "crx,irx->ci",
                    upstream,
                    padded[:, row_tap : row_tap + out_rows, col_tap : col_tap + out_cols],
                    preferred_element_type=jnp.float32,
                )
            )
        tap_rows.append(jnp.stack(tap_cols))
    return jnp.stack(tap_rows)


def silu_slope(values):
    sigmoid = jax.nn.sigmoid(values)
    return sigmoid * (1.0 + values * (1.0 - sigmoid))


def per_device(
    stokes_q,
    stokes_u,
    wiener_filter,
    inverse_filter,
    lens_norm,
    conv_first,
    bias_first,
    conv_second,
    bias_second,
    head_weight,
    head_bias,
    cotangent,
):
    row_count, col_count = stokes_q.shape
    devices = lax.axis_size("row")
    height = row_count * devices
    pencil = col_count // devices
    band_cols = cotangent.shape[2]
    column_ids = lax.axis_index("row") * pencil + jnp.arange(pencil, dtype=jnp.int32)
    col_freq = wavenumber(column_ids, col_count)[None, :]
    row_freq = wavenumber(jnp.arange(height, dtype=jnp.int32), height)[:, None]
    radius = col_freq * col_freq + row_freq * row_freq
    safe_radius = jnp.where(radius > 0, radius, 1.0)
    cos_twice = (col_freq * col_freq - row_freq * row_freq) / safe_radius
    sin_twice = 2.0 * col_freq * row_freq / safe_radius
    stokes_spec = forward_grid(jnp.stack([stokes_q, stokes_u]))
    emode = cos_twice * stokes_spec[0] + sin_twice * stokes_spec[1]
    wiener_mode = wiener_filter * emode
    packed = inverse_filter * emode - col_freq * wiener_mode
    slope_y = lax.complex(-row_freq * jnp.imag(wiener_mode), row_freq * jnp.real(wiener_mode))
    fields = inverse_grid(jnp.stack([packed, slope_y]))
    filtered = jnp.real(fields[0])
    gradient_x = jnp.imag(fields[0])
    gradient_y = jnp.real(fields[1])
    power = forward_grid(jnp.stack([filtered * gradient_x, filtered * gradient_y]))
    mixed = col_freq * power[0] + row_freq * power[1]
    lens_spec = lax.complex(lens_norm * jnp.imag(mixed), -lens_norm * jnp.real(mixed))
    lens_real = jnp.real(inverse_grid(lens_spec[None])[0])
    band_start = col_count // 2 - band_cols // 2
    band_q = stokes_q[:, band_start : band_start + band_cols]
    band_u = stokes_u[:, band_start : band_start + band_cols]
    stokes_wide = row_rim(jnp.stack([band_q, band_u]).astype(jnp.bfloat16), 3)
    cotangent_wide = row_rim(cotangent, 1)
    lens_band = lens_real[:, band_start : band_start + band_cols]
    lens_wide = row_rim(lens_band.astype(jnp.bfloat16)[None], 3)
    input_wide = jnp.concatenate([lens_wide, stokes_wide], axis=0)
    input_taps = tap_stack(input_wide)
    first_matrix = conv_first.transpose(2, 0, 1, 3).reshape(conv_first.shape[2], -1)
    pre_first = (
        jnp.einsum(
            "ck,krx->crx", first_matrix, input_taps, preferred_element_type=jnp.float32
        )
        + bias_first[:, None, None]
    )
    global_rows = lax.axis_index("row") * row_count + jnp.arange(-2, row_count + 2)
    inside = (global_rows >= 0) & (global_rows < height)
    hidden_wide = jnp.where(inside[None, :, None], jax.nn.silu(pre_first), 0.0).astype(
        jnp.bfloat16
    )
    pre_second = conv_taps(hidden_wide, conv_second) + bias_second[:, None, None]
    hidden_second = jax.nn.silu(pre_second[:, 1:-1]).astype(jnp.bfloat16)
    head_out = jnp.einsum(
        "oc,crx->orx", head_weight, hidden_second, preferred_element_type=jnp.float32
    )
    delensed = jnp.stack([band_q, band_u]) + head_out + head_bias[:, None, None]
    grad_head = jnp.einsum(
        "orx,crx->oc", cotangent, hidden_second, preferred_element_type=jnp.float32
    )
    grad_head_bias = jnp.sum(cotangent.astype(jnp.float32), axis=(1, 2))
    through_head = jnp.einsum(
        "oc,orx->crx", head_weight, cotangent_wide, preferred_element_type=jnp.float32
    )
    back_wide = (through_head * silu_slope(pre_second)).astype(jnp.bfloat16)
    back_second = back_wide[:, 1:-1]
    grad_conv_second = kernel_grad(back_second, hidden_wide[:, 1:-1])
    grad_bias_second = jnp.sum(back_second.astype(jnp.float32), axis=(1, 2))
    back_first = (
        conv_back(back_wide, conv_second) * silu_slope(pre_first[:, 2:-2])
    ).astype(jnp.bfloat16)
    first_grad = jnp.einsum(
        "crx,krx->ck",
        back_first,
        input_taps[:, 2 : 2 + row_count],
        preferred_element_type=jnp.float32,
    )
    grad_conv_first = first_grad.reshape(conv_first.shape[2], 3, 3, -1).transpose(1, 2, 0, 3)
    grad_bias_first = jnp.sum(back_first.astype(jnp.float32), axis=(1, 2))
    summed = flat_sum(
        (
            grad_conv_second,
            grad_conv_first,
            grad_bias_first,
            grad_bias_second,
            grad_head,
            grad_head_bias,
        )
    )
    return (delensed, summed[1], summed[2], summed[0], *summed[3:])


def solution(mesh):
    return jax.shard_map(
        per_device,
        mesh=mesh,
        in_specs=(
            P(("patch", "row"), None),
            P(("patch", "row"), None),
            P("patch", "row"),
            P("patch", "row"),
            P("patch", "row"),
            P(),
            P(),
            P(),
            P(),
            P(),
            P(),
            P(None, ("patch", "row"), None),
        ),
        out_specs=(
            P(None, ("patch", "row"), None),
            P("patch", None, None, None),
            P("patch"),
            P("patch", None, None, None),
            P("patch"),
            P("patch", None),
            P("patch"),
        ),
        check_vma=False,
    )
```

```python
import jax
import jax.numpy as jnp
from jax import lax
from jax.sharding import PartitionSpec as P

LINK = jnp.bfloat16


def padded_2(block, sides, width):
    for axis, dim in sides:
        count = lax.axis_size(axis)
        forward = [(i, i + 1) for i in range(count - 1)]
        backward = [(target, source) for source, target in forward]
        low = lax.ppermute(
            lax.slice_in_dim(block, block.shape[dim] - width, None, axis=dim), axis, forward
        )
        high = lax.ppermute(lax.slice_in_dim(block, 0, width, axis=dim), axis, backward)
        block = jnp.concatenate([low, block, high], axis=dim)
    return block


def wavenumber(position, length):
    middle = length // 2
    shifted = jnp.where(
        position < middle, position, jnp.where(position == middle, 0, position - length)
    )
    return shifted.astype(jnp.float32) * (2.0 / length)


def to_pencils(spectra):
    count, rows, cols = spectra.shape
    devices = lax.axis_size("row")
    planes = jnp.concatenate([jnp.real(spectra), jnp.imag(spectra)], axis=0).astype(LINK)
    blocks = planes.reshape(2 * count, rows, devices, cols // devices).transpose(2, 0, 1, 3)
    arrived = lax.all_to_all(blocks, "row", split_axis=0, concat_axis=0, tiled=True)
    arrived = arrived.transpose(1, 0, 2, 3).reshape(2 * count, devices * rows, cols // devices)
    arrived = arrived.astype(jnp.float32)
    return lax.complex(arrived[:count], arrived[count:])


def to_rows(spectra):
    count = spectra.shape[0]
    planes = jnp.concatenate([jnp.real(spectra), jnp.imag(spectra)], axis=0).astype(LINK)
    arrived = lax.all_to_all(planes, "row", split_axis=1, concat_axis=2, tiled=True)
    arrived = arrived.astype(jnp.float32)
    return lax.complex(arrived[:count], arrived[count:])


def butterfly_sum(values, axis):
    count = lax.axis_size(axis)
    if count & (count - 1):
        return lax.psum(values, axis)
    index = lax.axis_index(axis)
    stride = 1
    while stride < count:
        radix = 4 if count % (stride * 4) == 0 else 2
        received = [values] + [
            lax.ppermute(values, axis, [(i, i ^ (k * stride)) for i in range(count)])
            for k in range(1, radix)
        ]
        digit = (index // stride) % radix
        ordered = jnp.take(
            jnp.stack(received), jnp.arange(radix, dtype=jnp.int32) ^ digit, axis=0
        )
        values = ordered[0]
        for k in range(1, radix):
            values = values + ordered[k]
        stride *= radix
    return values


def flat_sum(tensors):
    flat = butterfly_sum(jnp.concatenate([t.reshape(-1) for t in tensors]), "row")
    summed = []
    offset = 0
    for t in tensors:
        summed.append(flat[offset : offset + t.size].reshape(t.shape))
        offset += t.size
    return summed


def forward_grid(fields):
    rows = jnp.fft.fft(fields.astype(jnp.complex64), axis=-1)
    return jnp.fft.fft(to_pencils(rows), axis=-2)


def inverse_grid(spectra):
    cols = jnp.fft.ifft(spectra, axis=-2)
    return jnp.fft.ifft(to_rows(cols), axis=-1)


def row_rim(block, depth):
    return padded_2(block, (("row", 1),), depth)


def pad_columns(block):
    return jnp.pad(block, ((0, 0), (0, 0), (1, 1)))


def tap_stack(rows_wide):
    out_rows = rows_wide.shape[1] - 2
    out_cols = rows_wide.shape[2]
    padded = pad_columns(rows_wide)
    return jnp.concatenate(
        [
            padded[:, row_tap : row_tap + out_rows, col_tap : col_tap + out_cols]
            for row_tap in range(3)
            for col_tap in range(3)
        ],
        axis=0,
    )


def conv_taps(rows_wide, kernel):
    out_rows = rows_wide.shape[1] - 2
    out_cols = rows_wide.shape[2]
    padded = pad_columns(rows_wide)
    summed = None
    for row_tap in range(3):
        for col_tap in range(3):
            partial_value = jnp.einsum(
                "ci,irx->crx",
                kernel[row_tap, col_tap],
                padded[:, row_tap : row_tap + out_rows, col_tap : col_tap + out_cols],
                preferred_element_type=jnp.float32,
            )
            summed = partial_value if summed is None else summed + partial_value
    return summed


def conv_back(rows_wide, kernel):
    out_rows = rows_wide.shape[1] - 2
    out_cols = rows_wide.shape[2]
    padded = pad_columns(rows_wide)
    summed = None
    for row_tap in range(3):
        for col_tap in range(3):
            partial_value = jnp.einsum(
                "ci,crx->irx",
                kernel[row_tap, col_tap],
                padded[
                    :, 2 - row_tap : 2 - row_tap + out_rows, 2 - col_tap : 2 - col_tap + out_cols
                ],
                preferred_element_type=jnp.float32,
            )
            summed = partial_value if summed is None else summed + partial_value
    return summed


def kernel_grad(upstream, rows_wide):
    out_rows = upstream.shape[1]
    out_cols = upstream.shape[2]
    padded = pad_columns(rows_wide)
    tap_rows = []
    for row_tap in range(3):
        tap_cols = []
        for col_tap in range(3):
            tap_cols.append(
                jnp.einsum(
                    "crx,irx->ci",
                    upstream,
                    padded[:, row_tap : row_tap + out_rows, col_tap : col_tap + out_cols],
                    preferred_element_type=jnp.float32,
                )
            )
        tap_rows.append(jnp.stack(tap_cols))
    return jnp.stack(tap_rows)


def silu_slope(values):
    sigmoid = jax.nn.sigmoid(values)
    return sigmoid * (1.0 + values * (1.0 - sigmoid))


def per_device(
    stokes_q,
    stokes_u,
    wiener_filter,
    inverse_filter,
    lens_norm,
    conv_first,
    bias_first,
    conv_second,
    bias_second,
    head_weight,
    head_bias,
    cotangent,
):
    row_count, col_count = stokes_q.shape
    devices = lax.axis_size("row")
    height = row_count * devices
    pencil = col_count // devices
    band_cols = cotangent.shape[2]
    column_ids = lax.axis_index("row") * pencil + jnp.arange(pencil, dtype=jnp.int32)
    col_freq = wavenumber(column_ids, col_count)[None, :]
    row_freq = wavenumber(jnp.arange(height, dtype=jnp.int32), height)[:, None]
    radius = col_freq * col_freq + row_freq * row_freq
    safe_radius = jnp.where(radius > 0, radius, 1.0)
    cos_twice = (col_freq * col_freq - row_freq * row_freq) / safe_radius
    sin_twice = 2.0 * col_freq * row_freq / safe_radius
    stokes_spec = forward_grid(jnp.stack([stokes_q, stokes_u]))
    emode = cos_twice * stokes_spec[0] + sin_twice * stokes_spec[1]
    wiener_mode = wiener_filter * emode
    packed = inverse_filter * emode - col_freq * wiener_mode
    slope_y = lax.complex(-row_freq * jnp.imag(wiener_mode), row_freq * jnp.real(wiener_mode))
    fields = inverse_grid(jnp.stack([packed, slope_y]))
    filtered = jnp.real(fields[0])
    gradient_x = jnp.imag(fields[0])
    gradient_y = jnp.real(fields[1])
    power = forward_grid(jnp.stack([filtered * gradient_x, filtered * gradient_y]))
    mixed = col_freq * power[0] + row_freq * power[1]
    lens_spec = lax.complex(lens_norm * jnp.imag(mixed), -lens_norm * jnp.real(mixed))
    lens_real = jnp.real(inverse_grid(lens_spec[None])[0])
    band_start = col_count // 2 - band_cols // 2
    band_q = stokes_q[:, band_start : band_start + band_cols]
    band_u = stokes_u[:, band_start : band_start + band_cols]
    stokes_wide = row_rim(jnp.stack([band_q, band_u]).astype(jnp.bfloat16), 3)
    cotangent_wide = row_rim(cotangent, 1)
    lens_band = lens_real[:, band_start : band_start + band_cols]
    lens_wide = row_rim(lens_band.astype(jnp.bfloat16)[None], 3)
    stokes_taps = tap_stack(stokes_wide)
    lens_taps = tap_stack(lens_wide)
    channels = conv_first.shape[2]
    stokes_matrix = conv_first[..., 1:].transpose(2, 0, 1, 3).reshape(channels, -1)
    lens_matrix = conv_first[..., :1].transpose(2, 0, 1, 3).reshape(channels, -1)
    stokes_part = jnp.einsum(
        "ck,krx->crx", stokes_matrix, stokes_taps, preferred_element_type=jnp.float32
    )
    pre_first = (
        jnp.einsum("ck,krx->crx", lens_matrix, lens_taps, preferred_element_type=jnp.float32)
        + stokes_part
        + bias_first[:, None, None]
    )
    global_rows = lax.axis_index("row") * row_count + jnp.arange(-2, row_count + 2)
    inside = (global_rows >= 0) & (global_rows < height)
    hidden_wide = jnp.where(inside[None, :, None], jax.nn.silu(pre_first), 0.0).astype(
        jnp.bfloat16
    )
    pre_second = conv_taps(hidden_wide, conv_second) + bias_second[:, None, None]
    hidden_second = jax.nn.silu(pre_second[:, 1:-1]).astype(jnp.bfloat16)
    head_out = jnp.einsum(
        "oc,crx->orx", head_weight, hidden_second, preferred_element_type=jnp.float32
    )
    delensed = jnp.stack([band_q, band_u]) + head_out + head_bias[:, None, None]
    grad_head = jnp.einsum(
        "orx,crx->oc", cotangent, hidden_second, preferred_element_type=jnp.float32
    )
    grad_head_bias = jnp.sum(cotangent.astype(jnp.float32), axis=(1, 2))
    through_head = jnp.einsum(
        "oc,orx->crx", head_weight, cotangent_wide, preferred_element_type=jnp.float32
    )
    back_wide = (through_head * silu_slope(pre_second)).astype(jnp.bfloat16)
    back_second = back_wide[:, 1:-1]
    grad_conv_second = kernel_grad(back_second, hidden_wide[:, 1:-1])
    grad_bias_second = jnp.sum(back_second.astype(jnp.float32), axis=(1, 2))
    back_first = (
        conv_back(back_wide, conv_second) * silu_slope(pre_first[:, 2:-2])
    ).astype(jnp.bfloat16)
    lens_grad = jnp.einsum(
        "crx,krx->ck",
        back_first,
        lens_taps[:, 2 : 2 + row_count],
        preferred_element_type=jnp.float32,
    )
    stokes_grad = jnp.einsum(
        "crx,krx->ck",
        back_first,
        stokes_taps[:, 2 : 2 + row_count],
        preferred_element_type=jnp.float32,
    )
    grad_conv_first = jnp.concatenate(
        [lens_grad.reshape(channels, 3, 3, 1), stokes_grad.reshape(channels, 3, 3, -1)], axis=3
    ).transpose(1, 2, 0, 3)
    grad_bias_first = jnp.sum(back_first.astype(jnp.float32), axis=(1, 2))
    summed = flat_sum(
        (
            grad_conv_second,
            grad_conv_first,
            grad_bias_first,
            grad_bias_second,
            grad_head,
            grad_head_bias,
        )
    )
    return (delensed, summed[1], summed[2], summed[0], *summed[3:])


def solution(mesh):
    return jax.shard_map(
        per_device,
        mesh=mesh,
        in_specs=(
            P(("patch", "row"), None),
            P(("patch", "row"), None),
            P("patch", "row"),
            P("patch", "row"),
            P("patch", "row"),
            P(),
            P(),
            P(),
            P(),
            P(),
            P(),
            P(None, ("patch", "row"), None),
        ),
        out_specs=(
            P(None, ("patch", "row"), None),
            P("patch", None, None, None),
            P("patch"),
            P("patch", None, None, None),
            P("patch"),
            P("patch", None),
            P("patch"),
        ),
        check_vma=False,
    )
```

```python
import jax
import jax.numpy as jnp
from jax import lax
from jax.sharding import PartitionSpec as P

LINK = jnp.bfloat16


def padded_2(block, sides, width):
    for axis, dim in sides:
        count = lax.axis_size(axis)
        forward = [(i, i + 1) for i in range(count - 1)]
        backward = [(target, source) for source, target in forward]
        low = lax.ppermute(
            lax.slice_in_dim(block, block.shape[dim] - width, None, axis=dim), axis, forward
        )
        high = lax.ppermute(lax.slice_in_dim(block, 0, width, axis=dim), axis, backward)
        block = jnp.concatenate([low, block, high], axis=dim)
    return block


def wavenumber(position, length):
    middle = length // 2
    shifted = jnp.where(
        position < middle, position, jnp.where(position == middle, 0, position - length)
    )
    return shifted.astype(jnp.float32) * (2.0 / length)


def to_pencils(spectra):
    count, rows, cols = spectra.shape
    devices = lax.axis_size("row")
    planes = jnp.concatenate([jnp.real(spectra), jnp.imag(spectra)], axis=0).astype(LINK)
    blocks = planes.reshape(2 * count, rows, devices, cols // devices).transpose(2, 0, 1, 3)
    arrived = lax.all_to_all(blocks, "row", split_axis=0, concat_axis=0, tiled=True)
    arrived = arrived.transpose(1, 0, 2, 3).reshape(2 * count, devices * rows, cols // devices)
    arrived = arrived.astype(jnp.float32)
    return lax.complex(arrived[:count], arrived[count:])


def to_rows(spectra):
    count = spectra.shape[0]
    planes = jnp.concatenate([jnp.real(spectra), jnp.imag(spectra)], axis=0).astype(LINK)
    arrived = lax.all_to_all(planes, "row", split_axis=1, concat_axis=2, tiled=True)
    arrived = arrived.astype(jnp.float32)
    return lax.complex(arrived[:count], arrived[count:])


def butterfly_sum(values, axis):
    count = lax.axis_size(axis)
    if count & (count - 1):
        return lax.psum(values, axis)
    index = lax.axis_index(axis)
    stride = 1
    while stride < count:
        radix = 4 if count % (stride * 4) == 0 else 2
        received = [values] + [
            lax.ppermute(values, axis, [(i, i ^ (k * stride)) for i in range(count)])
            for k in range(1, radix)
        ]
        digit = (index // stride) % radix
        ordered = jnp.take(
            jnp.stack(received), jnp.arange(radix, dtype=jnp.int32) ^ digit, axis=0
        )
        values = ordered[0]
        for k in range(1, radix):
            values = values + ordered[k]
        stride *= radix
    return values


def flat_sum(tensors):
    flat = butterfly_sum(jnp.concatenate([t.reshape(-1) for t in tensors]), "row")
    summed = []
    offset = 0
    for t in tensors:
        summed.append(flat[offset : offset + t.size].reshape(t.shape))
        offset += t.size
    return summed


def forward_grid(fields):
    rows = jnp.fft.fft(fields.astype(jnp.complex64), axis=-1)
    return jnp.fft.fft(to_pencils(rows), axis=-2)


def inverse_grid(spectra):
    cols = jnp.fft.ifft(spectra, axis=-2)
    return jnp.fft.ifft(to_rows(cols), axis=-1)


def row_rim(block, depth):
    return padded_2(block, (("row", 1),), depth)


def pad_columns(block):
    return jnp.pad(block, ((0, 0), (0, 0), (1, 1)))


def tap_stack(rows_wide):
    out_rows = rows_wide.shape[1] - 2
    out_cols = rows_wide.shape[2]
    padded = pad_columns(rows_wide)
    return jnp.concatenate(
        [
            padded[:, row_tap : row_tap + out_rows, col_tap : col_tap + out_cols]
            for row_tap in range(3)
            for col_tap in range(3)
        ],
        axis=0,
    )


def conv_taps(rows_wide, kernel):
    out_rows = rows_wide.shape[1] - 2
    out_cols = rows_wide.shape[2]
    padded = pad_columns(rows_wide)
    summed = None
    for row_tap in range(3):
        for col_tap in range(3):
            partial_value = jnp.einsum(
                "ci,irx->crx",
                kernel[row_tap, col_tap],
                padded[:, row_tap : row_tap + out_rows, col_tap : col_tap + out_cols],
                preferred_element_type=jnp.float32,
            )
            summed = partial_value if summed is None else summed + partial_value
    return summed


def conv_back(rows_wide, kernel):
    out_rows = rows_wide.shape[1] - 2
    out_cols = rows_wide.shape[2]
    padded = pad_columns(rows_wide)
    summed = None
    for row_tap in range(3):
        for col_tap in range(3):
            partial_value = jnp.einsum(
                "ci,crx->irx",
                kernel[row_tap, col_tap],
                padded[
                    :, 2 - row_tap : 2 - row_tap + out_rows, 2 - col_tap : 2 - col_tap + out_cols
                ],
                preferred_element_type=jnp.float32,
            )
            summed = partial_value if summed is None else summed + partial_value
    return summed


def kernel_grad(upstream, rows_wide):
    out_rows = upstream.shape[1]
    out_cols = upstream.shape[2]
    padded = pad_columns(rows_wide)
    tap_rows = []
    for row_tap in range(3):
        tap_cols = []
        for col_tap in range(3):
            tap_cols.append(
                jnp.einsum(
                    "crx,irx->ci",
                    upstream,
                    padded[:, row_tap : row_tap + out_rows, col_tap : col_tap + out_cols],
                    preferred_element_type=jnp.float32,
                )
            )
        tap_rows.append(jnp.stack(tap_cols))
    return jnp.stack(tap_rows)


def silu_slope(values):
    sigmoid = jax.nn.sigmoid(values)
    return sigmoid * (1.0 + values * (1.0 - sigmoid))


def per_device(
    stokes_q,
    stokes_u,
    wiener_filter,
    inverse_filter,
    lens_norm,
    conv_first,
    bias_first,
    conv_second,
    bias_second,
    head_weight,
    head_bias,
    cotangent,
):
    row_count, col_count = stokes_q.shape
    devices = lax.axis_size("row")
    height = row_count * devices
    pencil = col_count // devices
    band_cols = cotangent.shape[2]
    column_ids = lax.axis_index("row") * pencil + jnp.arange(pencil, dtype=jnp.int32)
    col_freq = wavenumber(column_ids, col_count)[None, :]
    row_freq = wavenumber(jnp.arange(height, dtype=jnp.int32), height)[:, None]
    radius = col_freq * col_freq + row_freq * row_freq
    safe_radius = jnp.where(radius > 0, radius, 1.0)
    cos_twice = (col_freq * col_freq - row_freq * row_freq) / safe_radius
    sin_twice = 2.0 * col_freq * row_freq / safe_radius
    stokes_spec = forward_grid(jnp.stack([stokes_q, stokes_u]))
    emode = cos_twice * stokes_spec[0] + sin_twice * stokes_spec[1]
    wiener_mode = wiener_filter * emode
    packed = inverse_filter * emode - col_freq * wiener_mode
    slope_y = lax.complex(-row_freq * jnp.imag(wiener_mode), row_freq * jnp.real(wiener_mode))
    fields = inverse_grid(jnp.stack([packed, slope_y]))
    filtered = jnp.real(fields[0])
    gradient_x = jnp.imag(fields[0])
    gradient_y = jnp.real(fields[1])
    power = forward_grid(jnp.stack([filtered * gradient_x, filtered * gradient_y]))
    mixed = col_freq * power[0] + row_freq * power[1]
    lens_spec = lax.complex(lens_norm * jnp.imag(mixed), -lens_norm * jnp.real(mixed))
    lens_real = jnp.real(inverse_grid(lens_spec[None])[0])
    band_start = col_count // 2 - band_cols // 2
    band_q = stokes_q[:, band_start : band_start + band_cols]
    band_u = stokes_u[:, band_start : band_start + band_cols]
    stokes_wide = row_rim(jnp.stack([band_q, band_u]).astype(jnp.bfloat16), 3)
    cotangent_wide = row_rim(cotangent, 1)
    lens_band = lens_real[:, band_start : band_start + band_cols]
    lens_wide = row_rim(lens_band.astype(jnp.bfloat16)[None], 3)
    input_wide = jnp.concatenate([lens_wide, stokes_wide], axis=0)
    input_taps = tap_stack(input_wide)
    first_matrix = conv_first.transpose(2, 0, 1, 3).reshape(conv_first.shape[2], -1)
    pre_first = (
        jnp.einsum(
            "ck,krx->crx", first_matrix, input_taps, preferred_element_type=jnp.float32
        )
        + bias_first[:, None, None]
    )
    global_rows = lax.axis_index("row") * row_count + jnp.arange(-2, row_count + 2)
    inside = (global_rows >= 0) & (global_rows < height)
    hidden_wide = jnp.where(inside[None, :, None], jax.nn.silu(pre_first), 0.0).astype(
        jnp.bfloat16
    )
    hidden_padded = pad_columns(hidden_wide)
    hidden_cols = jnp.concatenate(
        [hidden_padded[:, :, col_tap : col_tap + band_cols] for col_tap in range(3)], axis=0
    )
    pre_second = bias_second[:, None, None]
    for row_tap in range(3):
        row_matrix = conv_second[row_tap].transpose(1, 0, 2).reshape(conv_second.shape[2], -1)
        pre_second = pre_second + jnp.einsum(
            "ck,krx->crx",
            row_matrix,
            hidden_cols[:, row_tap : row_tap + row_count + 2],
            preferred_element_type=jnp.float32,
        )
    hidden_second = jax.nn.silu(pre_second[:, 1:-1]).astype(jnp.bfloat16)
    head_out = jnp.einsum(
        "oc,crx->orx", head_weight, hidden_second, preferred_element_type=jnp.float32
    )
    delensed = jnp.stack([band_q, band_u]) + head_out + head_bias[:, None, None]
    grad_head = jnp.einsum(
        "orx,crx->oc", cotangent, hidden_second, preferred_element_type=jnp.float32
    )
    grad_head_bias = jnp.sum(cotangent.astype(jnp.float32), axis=(1, 2))
    through_head = jnp.einsum(
        "oc,orx->crx", head_weight, cotangent_wide, preferred_element_type=jnp.float32
    )
    back_wide = (through_head * silu_slope(pre_second)).astype(jnp.bfloat16)
    back_second = back_wide[:, 1:-1]
    grad_conv_second = kernel_grad(back_second, hidden_wide[:, 1:-1])
    grad_bias_second = jnp.sum(back_second.astype(jnp.float32), axis=(1, 2))
    back_first = (
        conv_back(back_wide, conv_second) * silu_slope(pre_first[:, 2:-2])
    ).astype(jnp.bfloat16)
    first_grad = jnp.einsum(
        "crx,krx->ck",
        back_first,
        input_taps[:, 2 : 2 + row_count],
        preferred_element_type=jnp.float32,
    )
    grad_conv_first = first_grad.reshape(conv_first.shape[2], 3, 3, -1).transpose(1, 2, 0, 3)
    grad_bias_first = jnp.sum(back_first.astype(jnp.float32), axis=(1, 2))
    summed = flat_sum(
        (
            grad_conv_second,
            grad_conv_first,
            grad_bias_first,
            grad_bias_second,
            grad_head,
            grad_head_bias,
        )
    )
    return (delensed, summed[1], summed[2], summed[0], *summed[3:])


def solution(mesh):
    return jax.shard_map(
        per_device,
        mesh=mesh,
        in_specs=(
            P(("patch", "row"), None),
            P(("patch", "row"), None),
            P("patch", "row"),
            P("patch", "row"),
            P("patch", "row"),
            P(),
            P(),
            P(),
            P(),
            P(),
            P(),
            P(None, ("patch", "row"), None),
        ),
        out_specs=(
            P(None, ("patch", "row"), None),
            P("patch", None, None, None),
            P("patch"),
            P("patch", None, None, None),
            P("patch"),
            P("patch", None),
            P("patch"),
        ),
        check_vma=False,
    )
```

```python
import jax
import jax.numpy as jnp
from jax import lax
from jax.sharding import PartitionSpec as P

LINK = jnp.bfloat16


def padded_2(block, sides, width):
    for axis, dim in sides:
        count = lax.axis_size(axis)
        forward = [(i, i + 1) for i in range(count - 1)]
        backward = [(target, source) for source, target in forward]
        low = lax.ppermute(
            lax.slice_in_dim(block, block.shape[dim] - width, None, axis=dim), axis, forward
        )
        high = lax.ppermute(lax.slice_in_dim(block, 0, width, axis=dim), axis, backward)
        block = jnp.concatenate([low, block, high], axis=dim)
    return block


def wavenumber(position, length):
    middle = length // 2
    shifted = jnp.where(
        position < middle, position, jnp.where(position == middle, 0, position - length)
    )
    return shifted.astype(jnp.float32) * (2.0 / length)


def to_pencils(spectra):
    count, rows, cols = spectra.shape
    devices = lax.axis_size("row")
    planes = jnp.concatenate([jnp.real(spectra), jnp.imag(spectra)], axis=0).astype(LINK)
    blocks = planes.reshape(2 * count, rows, devices, cols // devices).transpose(2, 0, 1, 3)
    arrived = lax.all_to_all(blocks, "row", split_axis=0, concat_axis=0, tiled=True)
    arrived = arrived.transpose(1, 0, 2, 3).reshape(2 * count, devices * rows, cols // devices)
    arrived = arrived.astype(jnp.float32)
    return lax.complex(arrived[:count], arrived[count:])


def to_rows(spectra):
    count = spectra.shape[0]
    planes = jnp.concatenate([jnp.real(spectra), jnp.imag(spectra)], axis=0).astype(LINK)
    arrived = lax.all_to_all(planes, "row", split_axis=1, concat_axis=2, tiled=True)
    arrived = arrived.astype(jnp.float32)
    return lax.complex(arrived[:count], arrived[count:])


def butterfly_sum(values, axis):
    count = lax.axis_size(axis)
    if count & (count - 1):
        return lax.psum(values, axis)
    index = lax.axis_index(axis)
    stride = 1
    while stride < count:
        radix = 4 if count % (stride * 4) == 0 else 2
        received = [values] + [
            lax.ppermute(values, axis, [(i, i ^ (k * stride)) for i in range(count)])
            for k in range(1, radix)
        ]
        digit = (index // stride) % radix
        ordered = jnp.take(
            jnp.stack(received), jnp.arange(radix, dtype=jnp.int32) ^ digit, axis=0
        )
        values = ordered[0]
        for k in range(1, radix):
            values = values + ordered[k]
        stride *= radix
    return values


def flat_sum(tensors):
    flat = butterfly_sum(jnp.concatenate([t.reshape(-1) for t in tensors]), "row")
    summed = []
    offset = 0
    for t in tensors:
        summed.append(flat[offset : offset + t.size].reshape(t.shape))
        offset += t.size
    return summed


def forward_grid(fields):
    rows = jnp.fft.fft(fields.astype(jnp.complex64), axis=-1)
    return jnp.fft.fft(to_pencils(rows), axis=-2)


def inverse_grid(spectra):
    cols = jnp.fft.ifft(spectra, axis=-2)
    return jnp.fft.ifft(to_rows(cols), axis=-1)


def row_rim(block, depth):
    return padded_2(block, (("row", 1),), depth)


def pad_columns(block):
    return jnp.pad(block, ((0, 0), (0, 0), (1, 1)))


def tap_stack(rows_wide):
    out_rows = rows_wide.shape[1] - 2
    out_cols = rows_wide.shape[2]
    padded = pad_columns(rows_wide)
    return jnp.concatenate(
        [
            padded[:, row_tap : row_tap + out_rows, col_tap : col_tap + out_cols]
            for row_tap in range(3)
            for col_tap in range(3)
        ],
        axis=0,
    )


def conv_taps(rows_wide, kernel):
    out_rows = rows_wide.shape[1] - 2
    out_cols = rows_wide.shape[2]
    padded = pad_columns(rows_wide)
    summed = None
    for row_tap in range(3):
        for col_tap in range(3):
            partial_value = jnp.einsum(
                "ci,irx->crx",
                kernel[row_tap, col_tap],
                padded[:, row_tap : row_tap + out_rows, col_tap : col_tap + out_cols],
                preferred_element_type=jnp.float32,
            )
            summed = partial_value if summed is None else summed + partial_value
    return summed


def conv_back(rows_wide, kernel):
    out_rows = rows_wide.shape[1] - 2
    out_cols = rows_wide.shape[2]
    padded = pad_columns(rows_wide)
    summed = None
    for row_tap in range(3):
        for col_tap in range(3):
            partial_value = jnp.einsum(
                "ci,crx->irx",
                kernel[row_tap, col_tap],
                padded[
                    :, 2 - row_tap : 2 - row_tap + out_rows, 2 - col_tap : 2 - col_tap + out_cols
                ],
                preferred_element_type=jnp.float32,
            )
            summed = partial_value if summed is None else summed + partial_value
    return summed


def back_through(rows_wide, kernel, cols, rows):
    padded = pad_columns(rows_wide)
    shifted = jnp.concatenate(
        [padded[:, :, 2 - col_tap : 2 - col_tap + cols] for col_tap in range(3)], axis=0
    )
    summed = None
    for row_tap in range(3):
        row_matrix = kernel[row_tap].transpose(2, 0, 1).reshape(kernel.shape[3], -1)
        partial_value = jnp.einsum(
            "ik,krx->irx",
            row_matrix,
            shifted[:, 2 - row_tap : 2 - row_tap + rows],
            preferred_element_type=jnp.float32,
        )
        summed = partial_value if summed is None else summed + partial_value
    return summed


def kernel_grad(upstream, rows_wide):
    out_rows = upstream.shape[1]
    out_cols = upstream.shape[2]
    padded = pad_columns(rows_wide)
    tap_rows = []
    for row_tap in range(3):
        tap_cols = []
        for col_tap in range(3):
            tap_cols.append(
                jnp.einsum(
                    "crx,irx->ci",
                    upstream,
                    padded[:, row_tap : row_tap + out_rows, col_tap : col_tap + out_cols],
                    preferred_element_type=jnp.float32,
                )
            )
        tap_rows.append(jnp.stack(tap_cols))
    return jnp.stack(tap_rows)


def silu_slope(values):
    sigmoid = jax.nn.sigmoid(values)
    return sigmoid * (1.0 + values * (1.0 - sigmoid))


def per_device(
    stokes_q,
    stokes_u,
    wiener_filter,
    inverse_filter,
    lens_norm,
    conv_first,
    bias_first,
    conv_second,
    bias_second,
    head_weight,
    head_bias,
    cotangent,
):
    row_count, col_count = stokes_q.shape
    devices = lax.axis_size("row")
    height = row_count * devices
    pencil = col_count // devices
    band_cols = cotangent.shape[2]
    column_ids = lax.axis_index("row") * pencil + jnp.arange(pencil, dtype=jnp.int32)
    col_freq = wavenumber(column_ids, col_count)[None, :]
    row_freq = wavenumber(jnp.arange(height, dtype=jnp.int32), height)[:, None]
    radius = col_freq * col_freq + row_freq * row_freq
    safe_radius = jnp.where(radius > 0, radius, 1.0)
    cos_twice = (col_freq * col_freq - row_freq * row_freq) / safe_radius
    sin_twice = 2.0 * col_freq * row_freq / safe_radius
    stokes_spec = forward_grid(jnp.stack([stokes_q, stokes_u]))
    emode = cos_twice * stokes_spec[0] + sin_twice * stokes_spec[1]
    wiener_mode = wiener_filter * emode
    packed = inverse_filter * emode - col_freq * wiener_mode
    slope_y = lax.complex(-row_freq * jnp.imag(wiener_mode), row_freq * jnp.real(wiener_mode))
    fields = inverse_grid(jnp.stack([packed, slope_y]))
    filtered = jnp.real(fields[0])
    gradient_x = jnp.imag(fields[0])
    gradient_y = jnp.real(fields[1])
    power = forward_grid(jnp.stack([filtered * gradient_x, filtered * gradient_y]))
    mixed = col_freq * power[0] + row_freq * power[1]
    lens_spec = lax.complex(lens_norm * jnp.imag(mixed), -lens_norm * jnp.real(mixed))
    lens_real = jnp.real(inverse_grid(lens_spec[None])[0])
    band_start = col_count // 2 - band_cols // 2
    band_q = stokes_q[:, band_start : band_start + band_cols]
    band_u = stokes_u[:, band_start : band_start + band_cols]
    stokes_wide = row_rim(jnp.stack([band_q, band_u]).astype(jnp.bfloat16), 3)
    cotangent_wide = row_rim(cotangent, 1)
    lens_band = lens_real[:, band_start : band_start + band_cols]
    lens_wide = row_rim(lens_band.astype(jnp.bfloat16)[None], 3)
    input_wide = jnp.concatenate([lens_wide, stokes_wide], axis=0)
    input_taps = tap_stack(input_wide)
    first_matrix = conv_first.transpose(2, 0, 1, 3).reshape(conv_first.shape[2], -1)
    pre_first = (
        jnp.einsum(
            "ck,krx->crx", first_matrix, input_taps, preferred_element_type=jnp.float32
        )
        + bias_first[:, None, None]
    )
    global_rows = lax.axis_index("row") * row_count + jnp.arange(-2, row_count + 2)
    inside = (global_rows >= 0) & (global_rows < height)
    hidden_wide = jnp.where(inside[None, :, None], jax.nn.silu(pre_first), 0.0).astype(
        jnp.bfloat16
    )
    hidden_padded = pad_columns(hidden_wide)
    hidden_cols = jnp.concatenate(
        [hidden_padded[:, :, col_tap : col_tap + band_cols] for col_tap in range(3)], axis=0
    )
    pre_second = bias_second[:, None, None]
    for row_tap in range(3):
        row_matrix = conv_second[row_tap].transpose(1, 0, 2).reshape(conv_second.shape[2], -1)
        pre_second = pre_second + jnp.einsum(
            "ck,krx->crx",
            row_matrix,
            hidden_cols[:, row_tap : row_tap + row_count + 2],
            preferred_element_type=jnp.float32,
        )
    hidden_second = jax.nn.silu(pre_second[:, 1:-1]).astype(jnp.bfloat16)
    head_out = jnp.einsum(
        "oc,crx->orx", head_weight, hidden_second, preferred_element_type=jnp.float32
    )
    delensed = jnp.stack([band_q, band_u]) + head_out + head_bias[:, None, None]
    grad_head = jnp.einsum(
        "orx,crx->oc", cotangent, hidden_second, preferred_element_type=jnp.float32
    )
    grad_head_bias = jnp.sum(cotangent.astype(jnp.float32), axis=(1, 2))
    through_head = jnp.einsum(
        "oc,orx->crx", head_weight, cotangent_wide, preferred_element_type=jnp.float32
    )
    back_wide = (through_head * silu_slope(pre_second)).astype(jnp.bfloat16)
    back_second = back_wide[:, 1:-1]
    grad_conv_second = kernel_grad(back_second, hidden_wide[:, 1:-1])
    grad_bias_second = jnp.sum(back_second.astype(jnp.float32), axis=(1, 2))
    back_first = (
        back_through(back_wide, conv_second, band_cols, row_count)
        * silu_slope(pre_first[:, 2:-2])
    ).astype(jnp.bfloat16)
    first_grad = jnp.einsum(
        "crx,krx->ck",
        back_first,
        input_taps[:, 2 : 2 + row_count],
        preferred_element_type=jnp.float32,
    )
    grad_conv_first = first_grad.reshape(conv_first.shape[2], 3, 3, -1).transpose(1, 2, 0, 3)
    grad_bias_first = jnp.sum(back_first.astype(jnp.float32), axis=(1, 2))
    summed = flat_sum(
        (
            grad_conv_second,
            grad_conv_first,
            grad_bias_first,
            grad_bias_second,
            grad_head,
            grad_head_bias,
        )
    )
    return (delensed, summed[1], summed[2], summed[0], *summed[3:])


def solution(mesh):
    return jax.shard_map(
        per_device,
        mesh=mesh,
        in_specs=(
            P(("patch", "row"), None),
            P(("patch", "row"), None),
            P("patch", "row"),
            P("patch", "row"),
            P("patch", "row"),
            P(),
            P(),
            P(),
            P(),
            P(),
            P(),
            P(None, ("patch", "row"), None),
        ),
        out_specs=(
            P(None, ("patch", "row"), None),
            P("patch", None, None, None),
            P("patch"),
            P("patch", None, None, None),
            P("patch"),
            P("patch", None),
            P("patch"),
        ),
        check_vma=False,
    )
```

```python
import jax
import jax.numpy as jnp
from jax import lax
from jax.sharding import PartitionSpec as P

LINK = jnp.bfloat16


def padded_2(block, sides, width):
    for axis, dim in sides:
        count = lax.axis_size(axis)
        forward = [(i, i + 1) for i in range(count - 1)]
        backward = [(target, source) for source, target in forward]
        low = lax.ppermute(
            lax.slice_in_dim(block, block.shape[dim] - width, None, axis=dim), axis, forward
        )
        high = lax.ppermute(lax.slice_in_dim(block, 0, width, axis=dim), axis, backward)
        block = jnp.concatenate([low, block, high], axis=dim)
    return block


def wavenumber(position, length):
    middle = length // 2
    shifted = jnp.where(
        position < middle, position, jnp.where(position == middle, 0, position - length)
    )
    return shifted.astype(jnp.float32) * (2.0 / length)


def to_pencils(spectra):
    count, rows, cols = spectra.shape
    devices = lax.axis_size("row")
    planes = jnp.concatenate([jnp.real(spectra), jnp.imag(spectra)], axis=0).astype(LINK)
    blocks = planes.reshape(2 * count, rows, devices, cols // devices).transpose(2, 0, 1, 3)
    arrived = lax.all_to_all(blocks, "row", split_axis=0, concat_axis=0, tiled=True)
    arrived = arrived.transpose(1, 0, 2, 3).reshape(2 * count, devices * rows, cols // devices)
    arrived = arrived.astype(jnp.float32)
    return lax.complex(arrived[:count], arrived[count:])


def to_rows(spectra):
    count = spectra.shape[0]
    planes = jnp.concatenate([jnp.real(spectra), jnp.imag(spectra)], axis=0).astype(LINK)
    arrived = lax.all_to_all(planes, "row", split_axis=1, concat_axis=2, tiled=True)
    arrived = arrived.astype(jnp.float32)
    return lax.complex(arrived[:count], arrived[count:])


def butterfly_sum(values, axis):
    count = lax.axis_size(axis)
    if count & (count - 1):
        return lax.psum(values, axis)
    index = lax.axis_index(axis)
    stride = 1
    while stride < count:
        radix = 4 if count % (stride * 4) == 0 else 2
        received = [values] + [
            lax.ppermute(values, axis, [(i, i ^ (k * stride)) for i in range(count)])
            for k in range(1, radix)
        ]
        digit = (index // stride) % radix
        ordered = jnp.take(
            jnp.stack(received), jnp.arange(radix, dtype=jnp.int32) ^ digit, axis=0
        )
        values = ordered[0]
        for k in range(1, radix):
            values = values + ordered[k]
        stride *= radix
    return values


def flat_sum(tensors):
    flat = butterfly_sum(jnp.concatenate([t.reshape(-1) for t in tensors]), "row")
    summed = []
    offset = 0
    for t in tensors:
        summed.append(flat[offset : offset + t.size].reshape(t.shape))
        offset += t.size
    return summed


def forward_grid(fields):
    rows = jnp.fft.fft(fields.astype(jnp.complex64), axis=-1)
    return jnp.fft.fft(to_pencils(rows), axis=-2)


def inverse_grid(spectra):
    cols = jnp.fft.ifft(spectra, axis=-2)
    return jnp.fft.ifft(to_rows(cols), axis=-1)


def row_rim(block, depth):
    return padded_2(block, (("row", 1),), depth)


def pad_columns(block):
    return jnp.pad(block, ((0, 0), (0, 0), (1, 1)))


def tap_stack(rows_wide):
    out_rows = rows_wide.shape[1] - 2
    out_cols = rows_wide.shape[2]
    padded = pad_columns(rows_wide)
    return jnp.concatenate(
        [
            padded[:, row_tap : row_tap + out_rows, col_tap : col_tap + out_cols]
            for row_tap in range(3)
            for col_tap in range(3)
        ],
        axis=0,
    )


def conv_taps(rows_wide, kernel):
    out_rows = rows_wide.shape[1] - 2
    out_cols = rows_wide.shape[2]
    padded = pad_columns(rows_wide)
    summed = None
    for row_tap in range(3):
        for col_tap in range(3):
            partial_value = jnp.einsum(
                "ci,irx->crx",
                kernel[row_tap, col_tap],
                padded[:, row_tap : row_tap + out_rows, col_tap : col_tap + out_cols],
                preferred_element_type=jnp.float32,
            )
            summed = partial_value if summed is None else summed + partial_value
    return summed


def conv_back(rows_wide, kernel):
    out_rows = rows_wide.shape[1] - 2
    out_cols = rows_wide.shape[2]
    padded = pad_columns(rows_wide)
    summed = None
    for row_tap in range(3):
        for col_tap in range(3):
            partial_value = jnp.einsum(
                "ci,crx->irx",
                kernel[row_tap, col_tap],
                padded[
                    :, 2 - row_tap : 2 - row_tap + out_rows, 2 - col_tap : 2 - col_tap + out_cols
                ],
                preferred_element_type=jnp.float32,
            )
            summed = partial_value if summed is None else summed + partial_value
    return summed


def kernel_grad(upstream, rows_wide):
    out_rows = upstream.shape[1]
    out_cols = upstream.shape[2]
    padded = pad_columns(rows_wide)
    tap_rows = []
    for row_tap in range(3):
        tap_cols = []
        for col_tap in range(3):
            tap_cols.append(
                jnp.einsum(
                    "crx,irx->ci",
                    upstream,
                    padded[:, row_tap : row_tap + out_rows, col_tap : col_tap + out_cols],
                    preferred_element_type=jnp.float32,
                )
            )
        tap_rows.append(jnp.stack(tap_cols))
    return jnp.stack(tap_rows)


def silu_slope(values):
    sigmoid = jax.nn.sigmoid(values)
    return sigmoid * (1.0 + values * (1.0 - sigmoid))


def per_device(
    stokes_q,
    stokes_u,
    wiener_filter,
    inverse_filter,
    lens_norm,
    conv_first,
    bias_first,
    conv_second,
    bias_second,
    head_weight,
    head_bias,
    cotangent,
):
    row_count, col_count = stokes_q.shape
    devices = lax.axis_size("row")
    height = row_count * devices
    pencil = col_count // devices
    band_cols = cotangent.shape[2]
    column_ids = lax.axis_index("row") * pencil + jnp.arange(pencil, dtype=jnp.int32)
    col_freq = wavenumber(column_ids, col_count)[None, :]
    row_freq = wavenumber(jnp.arange(height, dtype=jnp.int32), height)[:, None]
    radius = col_freq * col_freq + row_freq * row_freq
    safe_radius = jnp.where(radius > 0, radius, 1.0)
    cos_twice = (col_freq * col_freq - row_freq * row_freq) / safe_radius
    sin_twice = 2.0 * col_freq * row_freq / safe_radius
    stokes_spec = forward_grid(jnp.stack([stokes_q, stokes_u]))
    emode = cos_twice * stokes_spec[0] + sin_twice * stokes_spec[1]
    wiener_mode = wiener_filter * emode
    packed = inverse_filter * emode - col_freq * wiener_mode
    slope_y = lax.complex(-row_freq * jnp.imag(wiener_mode), row_freq * jnp.real(wiener_mode))
    fields = inverse_grid(jnp.stack([packed, slope_y]))
    filtered = jnp.real(fields[0])
    gradient_x = jnp.imag(fields[0])
    gradient_y = jnp.real(fields[1])
    power = forward_grid(jnp.stack([filtered * gradient_x, filtered * gradient_y]))
    mixed = col_freq * power[0] + row_freq * power[1]
    lens_spec = lax.complex(lens_norm * jnp.imag(mixed), -lens_norm * jnp.real(mixed))
    lens_real = jnp.real(inverse_grid(lens_spec[None])[0])
    band_start = col_count // 2 - band_cols // 2
    band_q = stokes_q[:, band_start : band_start + band_cols]
    band_u = stokes_u[:, band_start : band_start + band_cols]
    stokes_wide = row_rim(jnp.stack([band_q, band_u]).astype(jnp.bfloat16), 3)
    cotangent_wide = row_rim(cotangent, 1)
    lens_band = lens_real[:, band_start : band_start + band_cols]
    lens_wide = row_rim(lens_band.astype(jnp.bfloat16)[None], 3)
    input_wide = jnp.concatenate([lens_wide, stokes_wide], axis=0)
    input_taps = tap_stack(input_wide)
    first_matrix = conv_first.transpose(2, 0, 1, 3).reshape(conv_first.shape[2], -1)
    pre_first = (
        jnp.einsum(
            "ck,krx->crx", first_matrix, input_taps, preferred_element_type=jnp.float32
        )
        + bias_first[:, None, None]
    )
    global_rows = lax.axis_index("row") * row_count + jnp.arange(-2, row_count + 2)
    inside = (global_rows >= 0) & (global_rows < height)
    hidden_wide = jnp.where(inside[None, :, None], jax.nn.silu(pre_first), 0.0).astype(
        jnp.bfloat16
    )
    hidden_padded = pad_columns(hidden_wide)
    hidden_cols = jnp.concatenate(
        [hidden_padded[:, :, col_tap : col_tap + band_cols] for col_tap in range(3)], axis=0
    )
    pre_second = bias_second[:, None, None]
    for row_tap in range(3):
        row_matrix = conv_second[row_tap].transpose(1, 0, 2).reshape(conv_second.shape[2], -1)
        pre_second = pre_second + jnp.einsum(
            "ck,krx->crx",
            row_matrix,
            hidden_cols[:, row_tap : row_tap + row_count + 2],
            preferred_element_type=jnp.float32,
        )
    hidden_second = jax.nn.silu(pre_second[:, 1:-1]).astype(jnp.bfloat16)
    head_out = jnp.einsum(
        "oc,crx->orx", head_weight, hidden_second, preferred_element_type=jnp.float32
    )
    delensed = jnp.stack([band_q, band_u]) + head_out + head_bias[:, None, None]
    grad_head = jnp.einsum(
        "orx,crx->oc", cotangent, hidden_second, preferred_element_type=jnp.float32
    )
    grad_head_bias = jnp.sum(cotangent.astype(jnp.float32), axis=(1, 2))
    through_head = jnp.einsum(
        "oc,orx->crx", head_weight, cotangent_wide, preferred_element_type=jnp.float32
    )
    back_wide = (through_head * silu_slope(pre_second)).astype(jnp.bfloat16)
    back_second = back_wide[:, 1:-1]
    grad_conv_second = jnp.stack(
        [
            jnp.einsum(
                "crx,krx->ck",
                back_second,
                hidden_cols[:, 1 + row_tap : 1 + row_tap + row_count],
                preferred_element_type=jnp.float32,
            )
            .reshape(back_second.shape[0], 3, -1)
            .transpose(1, 0, 2)
            for row_tap in range(3)
        ]
    )
    grad_bias_second = jnp.sum(back_second.astype(jnp.float32), axis=(1, 2))
    back_first = (
        conv_back(back_wide, conv_second) * silu_slope(pre_first[:, 2:-2])
    ).astype(jnp.bfloat16)
    first_grad = jnp.einsum(
        "crx,krx->ck",
        back_first,
        input_taps[:, 2 : 2 + row_count],
        preferred_element_type=jnp.float32,
    )
    grad_conv_first = first_grad.reshape(conv_first.shape[2], 3, 3, -1).transpose(1, 2, 0, 3)
    grad_bias_first = jnp.sum(back_first.astype(jnp.float32), axis=(1, 2))
    summed = flat_sum(
        (
            grad_conv_second,
            grad_conv_first,
            grad_bias_first,
            grad_bias_second,
            grad_head,
            grad_head_bias,
        )
    )
    return (delensed, summed[1], summed[2], summed[0], *summed[3:])


def solution(mesh):
    return jax.shard_map(
        per_device,
        mesh=mesh,
        in_specs=(
            P(("patch", "row"), None),
            P(("patch", "row"), None),
            P("patch", "row"),
            P("patch", "row"),
            P("patch", "row"),
            P(),
            P(),
            P(),
            P(),
            P(),
            P(),
            P(None, ("patch", "row"), None),
        ),
        out_specs=(
            P(None, ("patch", "row"), None),
            P("patch", None, None, None),
            P("patch"),
            P("patch", None, None, None),
            P("patch"),
            P("patch", None),
            P("patch"),
        ),
        check_vma=False,
    )
```
